128 devices in a mesh: section: 4 (over y), row: 4 (over z), col: 8 (over x, core).
Axes of the slice: x: 4, y: 4, z: 4, core: 2. Of those that a mesh axis runs over, the one named last changes fastest.
Arguments:
- block_input: float32 [4, 4, 256, 16, 1024], P('section', None, None, 'row', 'col'), may hold values from -6 to 6
- grad_out: float32 [4, 256, 16, 1024], P(None, None, 'row', 'col'), may hold values from -6 to 6
- w_reduce: float32 [4, 256, 64], P('section'), may hold values from -0.375 to 0.375
- w_spatial: float32 [4, 3, 3, 64, 64], P('section'), may hold values from -0.25 to 0.25
- w_expand: float32 [4, 64, 256], P('section'), may hold values from -0.75 to 0.75
- scale_one: float32 [4, 64], P('section'), may hold values from 0.1 to 1.9
- shift_one: float32 [4, 64], P('section'), may hold values from -3 to 3
- scale_two: float32 [4, 64], P('section'), may hold values from 0.1 to 1.9
- shift_two: float32 [4, 64], P('section'), may hold values from -3 to 3
- scale_three: float32 [4, 256], P('section'), may hold values from 0.1 to 1.9
- shift_three: float32 [4, 256], P('section'), may hold values from -3 to 3
Outputs:
- input_grads: float32 [4, 4, 256, 16, 1024], P('section', None, None, 'row', 'col')
- reduce_grad: float32 [4, 256, 64], P('section')
- spatial_grad: float32 [4, 3, 3, 64, 64], P('section')
- expand_grad: float32 [4, 64, 256], P('section')
The draws below stay inside these ranges and needn't reach their ends.
All inputs are finite; a program needn't handle non-finite values.
Results may differ from the reference program's by a relative error of at most 0.00026.
Values sent between devices are 32-bit elements; how exact they have to be, the bound alone decides.
No kernel may reach another device: no remote copies, remote signals or barrier semaphores. Data moves between devices by JAX's collectives and lax.ppermute only.
A program may use at most 128 MiB of HBM per device.

```python
import jax
import jax.numpy as jnp
from jax import lax

C = 256
M = 64
IMAGES = 4
SECTIONS = 4
ROWS = 16
COLS = 1024


def level_of(rng, shape, cuts, smallest, high):
    def one(dim, parts):
        heights = jax.random.uniform(jax.random.fold_in(jax.random.fold_in(rng, 6), dim), (parts,), jnp.float32, smallest / len(cuts), high / len(cuts))
        return jnp.repeat(jnp.exp(heights), shape[dim] // parts).reshape((-1,) + (1,) * (len(shape) - dim - 1))

    gain = one(*cuts[0])
    for cut in cuts[1:]:
        gain = gain * one(*cut)
    return gain


def gaussian(stream_key, dims, width, limit, cuts=(), held_as=jnp.bfloat16):
    result = jax.random.normal(stream_key, dims, jnp.float32) * width
    if len(cuts) > 0:
        result = level_of(stream_key, dims, cuts, -0.22, 0.18) * result
    return jnp.clip(result, min=-limit, max=limit).astype(held_as)


def setup_inputs(seed: int = 0) -> dict:
    splits = jax.random.split(jax.random.key(seed), 12)
    block_input = gaussian(splits[0], (SECTIONS, IMAGES, C, ROWS, COLS), 1.0, 6.0, ((0, 4), (3, 4), (4, 8)), jnp.float32)
    grad_out = gaussian(splits[1], (IMAGES, C, ROWS, COLS), 1.0, 6.0, ((2, 4), (3, 8)), jnp.float32)
    w_reduce = gaussian(splits[2], (SECTIONS, C, M), C ** -0.5, 0.375, ((0, 4),), jnp.float32)
    w_spatial = gaussian(splits[3], (SECTIONS, 3, 3, M, M), (9 * M) ** -0.5, 0.25, ((0, 4),), jnp.float32)
    w_expand = gaussian(splits[4], (SECTIONS, M, C), M ** -0.5, 0.75, ((0, 4),), jnp.float32)
    scale_one = jnp.clip(1.0 + 0.18 * jax.random.normal(splits[5], (SECTIONS, M), jnp.float32), 0.1, 1.9)
    shift_one = gaussian(splits[6], (SECTIONS, M), 0.5, 3.0, ((0, 4),), jnp.float32)
    scale_two = jnp.clip(1.0 + 0.18 * jax.random.normal(splits[7], (SECTIONS, M), jnp.float32), 0.1, 1.9)
    shift_two = gaussian(splits[8], (SECTIONS, M), 0.5, 3.0, ((0, 4),), jnp.float32)
    scale_three = jnp.clip(1.0 + 0.18 * jax.random.normal(splits[9], (SECTIONS, C), jnp.float32), 0.1, 1.9)
    shift_three = gaussian(splits[10], (SECTIONS, C), 0.5, 3.0, ((0, 4),), jnp.float32)
    return dict(block_input=block_input, grad_out=grad_out, w_reduce=w_reduce, w_spatial=w_spatial, w_expand=w_expand, scale_one=scale_one, shift_one=shift_one, scale_two=scale_two, shift_two=shift_two, scale_three=scale_three, shift_three=shift_three)


highest = lax.Precision.HIGHEST

def silu_grad(values):
    sig = jax.nn.sigmoid(values)
    return sig * (1.0 + values * (1.0 - sig))

def pointwise(values, weight):
    return jnp.einsum('nchw,cm->nmhw', values, weight, precision=highest)

def pointwise_back(values, weight):
    return jnp.einsum('nmhw,cm->nchw', values, weight, precision=highest)

def pad_cells(values):
    return jnp.pad(values, ((0, 0), (0, 0), (1, 1), (1, 1)))

def spatial(padded, weight, height, breadth):
    total = jnp.zeros((padded.shape[0], weight.shape[3], height, breadth), jnp.float32)
    for offset_row in range(3):
        for offset_col in range(3):
            piece = padded[:, :, offset_row:offset_row + height, offset_col:offset_col + breadth]
            total = total + pointwise(piece, weight[offset_row, offset_col])
    return total

def spatial_back(padded, weight, height, breadth):
    total = jnp.zeros((padded.shape[0], weight.shape[2], height, breadth), jnp.float32)
    for offset_row in range(3):
        for offset_col in range(3):
            piece = padded[:, :, 2 - offset_row:2 - offset_row + height, 2 - offset_col:2 - offset_col + breadth]
            total = total + pointwise_back(piece, weight[offset_row, offset_col])
    return total

def spatial_weight(padded, grad_second, height, breadth):
    rows_out = []
    for offset_row in range(3):
        cols_out = []
        for offset_col in range(3):
            piece = padded[:, :, offset_row:offset_row + height, offset_col:offset_col + breadth]
            cols_out.append(jnp.einsum('nchw,nohw->co', piece, grad_second, precision=highest))
        rows_out.append(jnp.stack(cols_out))
    return jnp.stack(rows_out)

def per_channel(values):
    return values[:, None, None]

def block_grad(inputs, upstream, w_reduce, w_spatial, w_expand, scale_one, shift_one, scale_two, shift_two, scale_three, shift_three):
    height, breadth = (inputs.shape[2], inputs.shape[3])
    first = pointwise(inputs, w_reduce) * per_channel(scale_one) + per_channel(shift_one)
    hidden_one = jax.nn.silu(first)
    padded_one = pad_cells(hidden_one)
    second = spatial(padded_one, w_spatial, height, breadth) * per_channel(scale_two) + per_channel(shift_two)
    hidden_two = jax.nn.silu(second)
    third = pointwise(hidden_two, w_expand) * per_channel(scale_three) + per_channel(shift_three)
    joined = inputs + third
    grad_joined = upstream * silu_grad(joined)
    grad_third = grad_joined * per_channel(scale_three)
    expand_term = jnp.einsum('nmhw,nchw->mc', hidden_two, grad_third, precision=highest)
    grad_second = pointwise_back(grad_third, w_expand) * silu_grad(second) * per_channel(scale_two)
    spatial_term = spatial_weight(padded_one, grad_second, height, breadth)
    grad_first = spatial_back(pad_cells(grad_second), w_spatial, height, breadth) * silu_grad(first) * per_channel(scale_one)
    reduce_term = jnp.einsum('nchw,nmhw->cm', inputs, grad_first, precision=highest)
    down_grad = grad_joined + pointwise_back(grad_first, w_reduce)
    return (down_grad, reduce_term, spatial_term, expand_term)

def reference(block_input, grad_out, w_reduce, w_spatial, w_expand, scale_one, shift_one, scale_two, shift_two, scale_three, shift_three):
    factor = 1.0 / jnp.sqrt(jnp.float32(IMAGES * ROWS * COLS))
    input_list = [None] * SECTIONS
    reduce_list = [None] * SECTIONS
    spatial_list = [None] * SECTIONS
    expand_list = [None] * SECTIONS
    upstream_all = grad_out
    for section_now in range(SECTIONS - 1, -1, -1):
        outs_down = []
        reduce_sum = jnp.zeros((C, M), jnp.float32)
        spatial_sum = jnp.zeros((3, 3, M, M), jnp.float32)
        expand_sum = jnp.zeros((M, C), jnp.float32)
        for image in range(IMAGES):
            down_grad, reduce_term, spatial_term, expand_term = block_grad(block_input[section_now, image:image + 1], upstream_all[image:image + 1], w_reduce[section_now], w_spatial[section_now], w_expand[section_now], scale_one[section_now], shift_one[section_now], scale_two[section_now], shift_two[section_now], scale_three[section_now], shift_three[section_now])
            outs_down.append(down_grad)
            reduce_sum = reduce_sum + reduce_term
            spatial_sum = spatial_sum + spatial_term
            expand_sum = expand_sum + expand_term
        upstream_all = jnp.concatenate(outs_down, axis=0)
        input_list[section_now] = upstream_all
        reduce_list[section_now] = reduce_sum * factor
        spatial_list[section_now] = spatial_sum * factor
        expand_list[section_now] = expand_sum * factor
    return (jnp.stack(input_list), jnp.stack(reduce_list), jnp.stack(spatial_list), jnp.stack(expand_list))
```

```python
import jax
import jax.numpy as jnp
from jax import lax
from jax.sharding import PartitionSpec as P

highest = lax.Precision.HIGHEST


def extended(value, sides, width):
    for axis, dim in sides:
        size, length = (lax.axis_size(axis), value.shape[dim])
        up = [(i, (i + 1) % size) for i in range(size - 1)]
        down = [(j, i) for i, j in up]
        last = lax.slice_in_dim(value, length - width, length, axis=dim)
        leading = lax.slice_in_dim(value, 0, width, axis=dim)
        before = lax.ppermute(last, axis, up)
        after = lax.ppermute(leading, axis, down)
        value = jnp.concatenate([before, value, after], axis=dim)
    return value


def silu_grad(values):
    sig = jax.nn.sigmoid(values)
    return sig * (1.0 + values * (1.0 - sig))


def pointwise(values, weight):
    return jnp.einsum("nchw,cm->nmhw", values, weight, precision=highest)


def pointwise_back(values, weight):
    return jnp.einsum("nmhw,cm->nchw", values, weight, precision=highest)


def spatial(padded, weight, height, breadth):
    total = jnp.zeros((padded.shape[0], weight.shape[3], height, breadth), jnp.float32)
    for offset_row in range(3):
        for offset_col in range(3):
            piece = padded[
                :, :, offset_row : offset_row + height, offset_col : offset_col + breadth
            ]
            total = total + pointwise(piece, weight[offset_row, offset_col])
    return total


def spatial_back(padded, weight, height, breadth):
    total = jnp.zeros((padded.shape[0], weight.shape[2], height, breadth), jnp.float32)
    for offset_row in range(3):
        for offset_col in range(3):
            piece = padded[
                :,
                :,
                2 - offset_row : 2 - offset_row + height,
                2 - offset_col : 2 - offset_col + breadth,
            ]
            total = total + pointwise_back(piece, weight[offset_row, offset_col])
    return total


def spatial_weight(padded, grad_second, height, breadth):
    rows_out = []
    for offset_row in range(3):
        cols_out = []
        for offset_col in range(3):
            piece = padded[
                :, :, offset_row : offset_row + height, offset_col : offset_col + breadth
            ]
            cols_out.append(jnp.einsum("nchw,nohw->co", piece, grad_second, precision=highest))
        rows_out.append(jnp.stack(cols_out))
    return jnp.stack(rows_out)


def per_channel(values):
    return values[:, None, None]


def forward(inputs, weights):
    w_reduce, w_spatial, w_expand, scale_one, shift_one, scale_two, shift_two, scale_three, shift_three = weights
    height, breadth = (inputs.shape[2], inputs.shape[3])
    first = pointwise(inputs, w_reduce) * per_channel(scale_one) + per_channel(shift_one)
    hidden_one = jax.nn.silu(first)
    padded_one = extended(hidden_one, (("row", 2), ("col", 3)), 1)
    second = spatial(padded_one, w_spatial, height, breadth) * per_channel(scale_two) + per_channel(
        shift_two
    )
    hidden_two = jax.nn.silu(second)
    third = pointwise(hidden_two, w_expand) * per_channel(scale_three) + per_channel(shift_three)
    joined = inputs + third
    return (first, padded_one, second, hidden_two, joined)


def backward(inputs, upstream, saved, weights):
    w_reduce, w_spatial, w_expand, scale_one, shift_one, scale_two, shift_two, scale_three, shift_three = weights
    first, padded_one, second, hidden_two, joined = saved
    height, breadth = (inputs.shape[2], inputs.shape[3])
    grad_joined = upstream * silu_grad(joined)
    grad_third = grad_joined * per_channel(scale_three)
    grad_second = pointwise_back(grad_third, w_expand) * silu_grad(second) * per_channel(scale_two)
    padded_grad = extended(grad_second, (("row", 2), ("col", 3)), 1)
    grad_first = (
        spatial_back(padded_grad, w_spatial, height, breadth)
        * silu_grad(first)
        * per_channel(scale_one)
    )
    down_grad = grad_joined + pointwise_back(grad_first, w_reduce)
    expand_term = jnp.einsum("nmhw,nchw->mc", hidden_two, grad_third, precision=highest)
    spatial_term = spatial_weight(padded_one, grad_second, height, breadth)
    reduce_term = jnp.einsum("nchw,nmhw->cm", inputs, grad_first, precision=highest)
    return down_grad, (reduce_term, spatial_term, expand_term)


def per_device(
    block_input,
    grad_out,
    w_reduce,
    w_spatial,
    w_expand,
    scale_one,
    shift_one,
    scale_two,
    shift_two,
    scale_three,
    shift_three,
):
    sections = lax.axis_size("section")
    me = lax.axis_index("section")
    images = block_input.shape[1]
    mine = lax.all_to_all(block_input[0], "section", 0, 0, tiled=True)
    gathered = [
        lax.all_gather(w[0], "section")
        for w in (
            w_reduce,
            w_spatial,
            w_expand,
            scale_one,
            shift_one,
            scale_two,
            shift_two,
            scale_three,
            shift_three,
        )
    ]
    per_image = images // sections
    upstream = lax.dynamic_slice_in_dim(grad_out, me * per_image, per_image, axis=0)
    cells = images * mine.shape[2] * mine.shape[3] * lax.axis_size("row") * lax.axis_size("col")
    factor = 1.0 / jnp.sqrt(jnp.float32(cells))
    down = [None] * sections
    terms = [None] * sections
    for sec in range(sections - 1, -1, -1):
        weights = tuple(g[sec] for g in gathered)
        inputs = mine[sec * per_image : (sec + 1) * per_image]
        saved = forward(inputs, weights)
        upstream, terms[sec] = backward(inputs, upstream, saved, weights)
        down[sec] = upstream
    results = lax.all_to_all(jnp.concatenate(down, axis=0), "section", 0, 0, tiled=True)
    sums = []
    for k in range(3):
        stacked = jnp.stack([terms[sec][k] for sec in range(sections)])
        total = lax.psum(stacked, ("section", "row", "col"))
        sums.append((lax.dynamic_index_in_dim(total, me, axis=0, keepdims=True) * factor))
    return (results[None], sums[0], sums[1], sums[2])


def solution(mesh):
    placed = (
        P("section", None, None, "row", "col"),
        P(None, None, "row", "col"),
        P("section", None, None),
        P("section", None, None, None, None),
        P("section", None, None),
        P("section", None),
        P("section", None),
        P("section", None),
        P("section", None),
        P("section", None),
        P("section", None),
    )
    return jax.shard_map(
        per_device,
        mesh=mesh,
        in_specs=placed,
        out_specs=(
            P("section", None, None, "row", "col"),
            P("section", None, None),
            P("section", None, None, None, None),
            P("section", None, None),
        ),
        check_vma=False,
    )
```

```python
import jax
import jax.numpy as jnp
from jax import lax
from jax.sharding import PartitionSpec as P

highest = lax.Precision.HIGHEST


def extended(value, sides, width):
    for axis, dim in sides:
        size, length = (lax.axis_size(axis), value.shape[dim])
        up = [(i, (i + 1) % size) for i in range(size - 1)]
        down = [(j, i) for i, j in up]
        last = lax.slice_in_dim(value, length - width, length, axis=dim)
        leading = lax.slice_in_dim(value, 0, width, axis=dim)
        before = lax.ppermute(last, axis, up)
        after = lax.ppermute(leading, axis, down)
        value = jnp.concatenate([before, value, after], axis=dim)
    return value


def silu_grad(values):
    sig = jax.nn.sigmoid(values)
    return sig * (1.0 + values * (1.0 - sig))


def pointwise(values, weight):
    return jnp.einsum("nchw,cm->nmhw", values, weight, precision=highest)


def pointwise_back(values, weight):
    return jnp.einsum("nmhw,cm->nchw", values, weight, precision=highest)


def spatial(padded, weight, height, breadth):
    total = jnp.zeros((padded.shape[0], weight.shape[3], height, breadth), jnp.float32)
    for offset_row in range(3):
        for offset_col in range(3):
            piece = padded[
                :, :, offset_row : offset_row + height, offset_col : offset_col + breadth
            ]
            total = total + pointwise(piece, weight[offset_row, offset_col])
    return total


def spatial_back(padded, weight, height, breadth):
    total = jnp.zeros((padded.shape[0], weight.shape[2], height, breadth), jnp.float32)
    for offset_row in range(3):
        for offset_col in range(3):
            piece = padded[
                :,
                :,
                2 - offset_row : 2 - offset_row + height,
                2 - offset_col : 2 - offset_col + breadth,
            ]
            total = total + pointwise_back(piece, weight[offset_row, offset_col])
    return total


def spatial_weight(padded, grad_second, height, breadth):
    rows_out = []
    for offset_row in range(3):
        cols_out = []
        for offset_col in range(3):
            piece = padded[
                :, :, offset_row : offset_row + height, offset_col : offset_col + breadth
            ]
            cols_out.append(jnp.einsum("nchw,nohw->co", piece, grad_second, precision=highest))
        rows_out.append(jnp.stack(cols_out))
    return jnp.stack(rows_out)


def per_channel(values):
    return values[:, None, None]


def forward(inputs, weights):
    w_reduce, w_spatial, w_expand, scale_one, shift_one, scale_two, shift_two, scale_three, shift_three = weights
    height, breadth = (inputs.shape[2], inputs.shape[3])
    first = pointwise(inputs, w_reduce) * per_channel(scale_one) + per_channel(shift_one)
    hidden_one = jax.nn.silu(first)
    padded_one = extended(hidden_one, (("row", 2), ("col", 3)), 1)
    second = spatial(padded_one, w_spatial, height, breadth) * per_channel(scale_two) + per_channel(
        shift_two
    )
    hidden_two = jax.nn.silu(second)
    third = pointwise(hidden_two, w_expand) * per_channel(scale_three) + per_channel(shift_three)
    joined = inputs + third
    return (first, padded_one, second, hidden_two, joined)


def backward(inputs, upstream, saved, weights):
    w_reduce, w_spatial, w_expand, scale_one, shift_one, scale_two, shift_two, scale_three, shift_three = weights
    first, padded_one, second, hidden_two, joined = saved
    height, breadth = (inputs.shape[2], inputs.shape[3])
    grad_joined = upstream * silu_grad(joined)
    grad_third = grad_joined * per_channel(scale_three)
    grad_second = pointwise_back(grad_third, w_expand) * silu_grad(second) * per_channel(scale_two)
    padded_grad = extended(grad_second, (("row", 2), ("col", 3)), 1)
    grad_first = (
        spatial_back(padded_grad, w_spatial, height, breadth)
        * silu_grad(first)
        * per_channel(scale_one)
    )
    down_grad = grad_joined + pointwise_back(grad_first, w_reduce)
    expand_term = jnp.einsum("nmhw,nchw->mc", hidden_two, grad_third, precision=highest)
    spatial_term = spatial_weight(padded_one, grad_second, height, breadth)
    reduce_term = jnp.einsum("nchw,nmhw->cm", inputs, grad_first, precision=highest)
    return down_grad, (reduce_term, spatial_term, expand_term)


def gathered_weights(weights, sections):
    flat = jnp.concatenate([w[0].reshape(-1) for w in weights])
    packed = jnp.broadcast_to(flat.reshape(1, -1, 128), (sections, flat.size // 128, 128))
    every = lax.all_to_all(packed, "section", 0, 0, tiled=True).reshape(sections, -1)
    out = []
    for sec in range(sections):
        offset, unpacked = (0, [])
        for w in weights:
            size = w[0].size
            unpacked.append(every[sec, offset : offset + size].reshape(w.shape[1:]))
            offset += size
        out.append(tuple(unpacked))
    return out


def reduced_terms(terms, sections):
    shapes = [t.shape for t in terms[0]]
    flat = jnp.stack([jnp.concatenate([t.reshape(-1) for t in ts]) for ts in terms])
    flat = flat.reshape(sections, -1, 128)
    by_image = lax.all_to_all(flat, "section", 0, 0, tiled=True).sum(axis=0)
    group = lax.axis_size("row") * lax.axis_size("col")
    pieces = by_image.reshape(group, -1, 128)
    mine = lax.all_to_all(pieces, ("row", "col"), 0, 0, tiled=True).sum(axis=0)
    copies = jnp.broadcast_to(mine[None], (group,) + mine.shape)
    total = lax.all_to_all(copies, ("row", "col"), 0, 0, tiled=True).reshape(-1)
    out, offset = ([], 0)
    for shape in shapes:
        size = 1
        for d in shape:
            size *= d
        out.append(total[offset : offset + size].reshape(shape))
        offset += size
    return out


def per_device(
    block_input,
    grad_out,
    w_reduce,
    w_spatial,
    w_expand,
    scale_one,
    shift_one,
    scale_two,
    shift_two,
    scale_three,
    shift_three,
):
    sections = lax.axis_size("section")
    me = lax.axis_index("section")
    images = block_input.shape[1]
    mine = lax.all_to_all(block_input[0], "section", 0, 0, tiled=True)
    gathered = gathered_weights(
        (w_reduce, w_spatial, w_expand, scale_one, shift_one, scale_two, shift_two, scale_three, shift_three),
        sections,
    )
    per_image = images // sections
    upstream = lax.dynamic_slice_in_dim(grad_out, me * per_image, per_image, axis=0)
    cells = images * mine.shape[2] * mine.shape[3] * lax.axis_size("row") * lax.axis_size("col")
    factor = 1.0 / jnp.sqrt(jnp.float32(cells))
    down = [None] * sections
    terms = [None] * sections
    for sec in range(sections - 1, -1, -1):
        weights = gathered[sec]
        inputs = mine[sec * per_image : (sec + 1) * per_image]
        saved = forward(inputs, weights)
        upstream, terms[sec] = backward(inputs, upstream, saved, weights)
        down[sec] = upstream
    results = lax.all_to_all(jnp.concatenate(down, axis=0), "section", 0, 0, tiled=True)
    sums = reduced_terms(terms, sections)
    return (results[None],) + tuple((t * factor)[None] for t in sums)


def solution(mesh):
    placed = (
        P("section", None, None, "row", "col"),
        P(None, None, "row", "col"),
        P("section", None, None),
        P("section", None, None, None, None),
        P("section", None, None),
        P("section", None),
        P("section", None),
        P("section", None),
        P("section", None),
        P("section", None),
        P("section", None),
    )
    return jax.shard_map(
        per_device,
        mesh=mesh,
        in_specs=placed,
        out_specs=(
            P("section", None, None, "row", "col"),
            P("section", None, None),
            P("section", None, None, None, None),
            P("section", None, None),
        ),
        check_vma=False,
    )
```

```python
import jax
import jax.numpy as jnp
from jax import lax
from jax.sharding import PartitionSpec as P

highest = lax.Precision.HIGHEST


def extended(value, sides, width):
    for axis, dim in sides:
        size, length = (lax.axis_size(axis), value.shape[dim])
        up = [(i, (i + 1) % size) for i in range(size - 1)]
        down = [(j, i) for i, j in up]
        last = lax.slice_in_dim(value, length - width, length, axis=dim)
        leading = lax.slice_in_dim(value, 0, width, axis=dim)
        before = lax.ppermute(last, axis, up)
        after = lax.ppermute(leading, axis, down)
        value = jnp.concatenate([before, value, after], axis=dim)
    return value


def silu_grad(values):
    sig = jax.nn.sigmoid(values)
    return sig * (1.0 + values * (1.0 - sig))


def pointwise(values, weight):
    return jnp.einsum("nchw,cm->nmhw", values, weight, precision=highest)


def pointwise_back(values, weight):
    return jnp.einsum("nmhw,cm->nchw", values, weight, precision=highest)


def spatial(padded, weight, height, breadth):
    total = jnp.zeros((padded.shape[0], weight.shape[3], height, breadth), jnp.float32)
    for offset_row in range(3):
        for offset_col in range(3):
            piece = padded[
                :, :, offset_row : offset_row + height, offset_col : offset_col + breadth
            ]
            total = total + pointwise(piece, weight[offset_row, offset_col])
    return total


def spatial_back(padded, weight, height, breadth):
    total = jnp.zeros((padded.shape[0], weight.shape[2], height, breadth), jnp.float32)
    for offset_row in range(3):
        for offset_col in range(3):
            piece = padded[
                :,
                :,
                2 - offset_row : 2 - offset_row + height,
                2 - offset_col : 2 - offset_col + breadth,
            ]
            total = total + pointwise_back(piece, weight[offset_row, offset_col])
    return total


def spatial_weight(padded, grad_second, height, breadth):
    rows_out = []
    for offset_row in range(3):
        cols_out = []
        for offset_col in range(3):
            piece = padded[
                :, :, offset_row : offset_row + height, offset_col : offset_col + breadth
            ]
            cols_out.append(jnp.einsum("nchw,nohw->co", piece, grad_second, precision=highest))
        rows_out.append(jnp.stack(cols_out))
    return jnp.stack(rows_out)


def per_channel(values):
    return values[:, None, None]


def stacked_channel(values):
    return values[:, :, None, None]


def forward(inputs, weights):
    w_reduce, w_spatial, w_expand, scale_one, shift_one, scale_two, shift_two, scale_three, shift_three = weights
    height, breadth = (inputs.shape[2], inputs.shape[3])
    first = jnp.einsum("nchw,ncm->nmhw", inputs, w_reduce, precision=highest)
    first = first * stacked_channel(scale_one) + stacked_channel(shift_one)
    hidden_one = jax.nn.silu(first)
    padded_one = extended(hidden_one, (("row", 2), ("col", 3)), 1)
    second = jnp.zeros((inputs.shape[0], w_spatial.shape[4], height, breadth), jnp.float32)
    for offset_row in range(3):
        for offset_col in range(3):
            piece = padded_one[
                :, :, offset_row : offset_row + height, offset_col : offset_col + breadth
            ]
            second = second + jnp.einsum(
                "nchw,ncm->nmhw", piece, w_spatial[:, offset_row, offset_col], precision=highest
            )
    second = second * stacked_channel(scale_two) + stacked_channel(shift_two)
    hidden_two = jax.nn.silu(second)
    third = jnp.einsum("nchw,ncm->nmhw", hidden_two, w_expand, precision=highest)
    third = third * stacked_channel(scale_three) + stacked_channel(shift_three)
    joined = inputs + third
    return (first, padded_one, second, hidden_two, joined)


def backward(inputs, upstream, saved, weights):
    w_reduce, w_spatial, w_expand, scale_one, shift_one, scale_two, shift_two, scale_three, shift_three = weights
    first, padded_one, second, hidden_two, joined = saved
    height, breadth = (inputs.shape[2], inputs.shape[3])
    grad_joined = upstream * silu_grad(joined)
    grad_third = grad_joined * per_channel(scale_three)
    grad_second = pointwise_back(grad_third, w_expand) * silu_grad(second) * per_channel(scale_two)
    padded_grad = extended(grad_second, (("row", 2), ("col", 3)), 1)
    grad_first = (
        spatial_back(padded_grad, w_spatial, height, breadth)
        * silu_grad(first)
        * per_channel(scale_one)
    )
    down_grad = grad_joined + pointwise_back(grad_first, w_reduce)
    expand_term = jnp.einsum("nmhw,nchw->mc", hidden_two, grad_third, precision=highest)
    spatial_term = spatial_weight(padded_one, grad_second, height, breadth)
    reduce_term = jnp.einsum("nchw,nmhw->cm", inputs, grad_first, precision=highest)
    return down_grad, (reduce_term, spatial_term, expand_term)


def gathered_weights(weights, sections):
    flat = jnp.concatenate([w[0].reshape(-1) for w in weights])
    packed = jnp.broadcast_to(flat.reshape(1, -1, 128), (sections, flat.size // 128, 128))
    every = lax.all_to_all(packed, "section", 0, 0, tiled=True).reshape(sections, -1)
    offset, unpacked = (0, [])
    for w in weights:
        size = w[0].size
        unpacked.append(every[:, offset : offset + size].reshape((sections,) + w.shape[1:]))
        offset += size
    return tuple(unpacked)


def scattered_terms(terms):
    flat = jnp.concatenate([t.reshape(-1) for t in terms]).reshape(-1, 128)
    for axis in ("col", "row"):
        size = lax.axis_size(axis)
        flat = lax.all_to_all(flat.reshape(size, -1, 128), axis, 0, 0, tiled=True).sum(axis=0)
    return flat


def reduced_terms(chunks, shapes, sections):
    stacked = jnp.stack(chunks)
    mine = lax.all_to_all(stacked, "section", 0, 0, tiled=True).sum(axis=0)
    for axis in ("row", "col"):
        size = lax.axis_size(axis)
        copies = jnp.broadcast_to(mine[None], (size,) + mine.shape)
        mine = lax.all_to_all(copies, axis, 0, 0, tiled=True).reshape(-1, 128)
    total = mine.reshape(-1)
    out, offset = ([], 0)
    for shape in shapes:
        size = 1
        for d in shape:
            size *= d
        out.append(total[offset : offset + size].reshape(shape))
        offset += size
    return out


def per_device(
    block_input,
    grad_out,
    w_reduce,
    w_spatial,
    w_expand,
    scale_one,
    shift_one,
    scale_two,
    shift_two,
    scale_three,
    shift_three,
):
    sections = lax.axis_size("section")
    me = lax.axis_index("section")
    images = block_input.shape[1]
    mine = lax.all_to_all(block_input[0], "section", 0, 0, tiled=True)
    gathered = gathered_weights(
        (w_reduce, w_spatial, w_expand, scale_one, shift_one, scale_two, shift_two, scale_three, shift_three),
        sections,
    )
    per_image = images // sections
    upstream = lax.dynamic_slice_in_dim(grad_out, me * per_image, per_image, axis=0)
    cells = images * mine.shape[2] * mine.shape[3] * lax.axis_size("row") * lax.axis_size("col")
    factor = 1.0 / jnp.sqrt(jnp.float32(cells))
    saved_all = forward(mine, gathered)
    down = [None] * sections
    chunks = [None] * sections
    shapes = None
    for sec in range(sections - 1, -1, -1):
        part = slice(sec * per_image, (sec + 1) * per_image)
        weights = tuple(g[sec] for g in gathered)
        saved = tuple(v[part] for v in saved_all)
        upstream, terms = backward(mine[part], upstream, saved, weights)
        shapes = [t.shape for t in terms]
        chunks[sec] = scattered_terms(terms)
        down[sec] = upstream
    results = lax.all_to_all(jnp.concatenate(down, axis=0), "section", 0, 0, tiled=True)
    sums = reduced_terms(chunks, shapes, sections)
    return (results[None],) + tuple((t * factor)[None] for t in sums)


def solution(mesh):
    placed = (
        P("section", None, None, "row", "col"),
        P(None, None, "row", "col"),
        P("section", None, None),
        P("section", None, None, None, None),
        P("section", None, None),
        P("section", None),
        P("section", None),
        P("section", None),
        P("section", None),
        P("section", None),
        P("section", None),
    )
    return jax.shard_map(
        per_device,
        mesh=mesh,
        in_specs=placed,
        out_specs=(
            P("section", None, None, "row", "col"),
            P("section", None, None),
            P("section", None, None, None, None),
            P("section", None, None),
        ),
        check_vma=False,
    )
```

```python
import jax
import jax.numpy as jnp
from jax import lax
from jax.sharding import PartitionSpec as P

highest = lax.Precision.HIGHEST


def extended(value, sides, width):
    for axis, dim in sides:
        size, length = (lax.axis_size(axis), value.shape[dim])
        up = [(i, (i + 1) % size) for i in range(size - 1)]
        down = [(j, i) for i, j in up]
        last = lax.slice_in_dim(value, length - width, length, axis=dim)
        leading = lax.slice_in_dim(value, 0, width, axis=dim)
        before = lax.ppermute(last, axis, up)
        after = lax.ppermute(leading, axis, down)
        value = jnp.concatenate([before, value, after], axis=dim)
    return value


def silu_grad(values):
    sig = jax.nn.sigmoid(values)
    return sig * (1.0 + values * (1.0 - sig))


def pointwise(values, weight):
    return jnp.einsum("nchw,cm->nmhw", values, weight, precision=highest)


def pointwise_back(values, weight):
    return jnp.einsum("nmhw,cm->nchw", values, weight, precision=highest)


def spatial(padded, weight, height, breadth):
    total = jnp.zeros((padded.shape[0], weight.shape[3], height, breadth), jnp.float32)
    for offset_row in range(3):
        for offset_col in range(3):
            piece = padded[
                :, :, offset_row : offset_row + height, offset_col : offset_col + breadth
            ]
            total = total + pointwise(piece, weight[offset_row, offset_col])
    return total


def spatial_back(padded, weight, height, breadth):
    total = jnp.zeros((padded.shape[0], weight.shape[2], height, breadth), jnp.float32)
    for offset_row in range(3):
        for offset_col in range(3):
            piece = padded[
                :,
                :,
                2 - offset_row : 2 - offset_row + height,
                2 - offset_col : 2 - offset_col + breadth,
            ]
            total = total + pointwise_back(piece, weight[offset_row, offset_col])
    return total


def spatial_weight(padded, grad_second, height, breadth):
    rows_out = []
    for offset_row in range(3):
        cols_out = []
        for offset_col in range(3):
            piece = padded[
                :, :, offset_row : offset_row + height, offset_col : offset_col + breadth
            ]
            cols_out.append(jnp.einsum("nchw,nohw->co", piece, grad_second, precision=highest))
        rows_out.append(jnp.stack(cols_out))
    return jnp.stack(rows_out)


def per_channel(values):
    return values[:, None, None]


def stacked_channel(values):
    return values[:, :, None, None]


def forward(inputs, weights):
    w_reduce, w_spatial, w_expand, scale_one, shift_one, scale_two, shift_two, scale_three, shift_three = weights
    height, breadth = (inputs.shape[2], inputs.shape[3])
    first = jnp.einsum("nchw,ncm->nmhw", inputs, w_reduce, precision=highest)
    first = first * stacked_channel(scale_one) + stacked_channel(shift_one)
    hidden_one = jax.nn.silu(first)
    padded_one = extended(hidden_one, (("row", 2), ("col", 3)), 1)
    second = jnp.zeros((inputs.shape[0], w_spatial.shape[4], height, breadth), jnp.float32)
    for offset_row in range(3):
        for offset_col in range(3):
            piece = padded_one[
                :, :, offset_row : offset_row + height, offset_col : offset_col + breadth
            ]
            second = second + jnp.einsum(
                "nchw,ncm->nmhw", piece, w_spatial[:, offset_row, offset_col], precision=highest
            )
    second = second * stacked_channel(scale_two) + stacked_channel(shift_two)
    hidden_two = jax.nn.silu(second)
    third = jnp.einsum("nchw,ncm->nmhw", hidden_two, w_expand, precision=highest)
    third = third * stacked_channel(scale_three) + stacked_channel(shift_three)
    joined = inputs + third
    return (first, padded_one, second, hidden_two, joined)


def backward(inputs, upstream, saved, weights):
    w_reduce, w_spatial, w_expand, scale_one, shift_one, scale_two, shift_two, scale_three, shift_three = weights
    first, padded_one, second, hidden_two, joined = saved
    height, breadth = (inputs.shape[2], inputs.shape[3])
    grad_joined = upstream * silu_grad(joined)
    grad_third = grad_joined * per_channel(scale_three)
    grad_second = pointwise_back(grad_third, w_expand) * silu_grad(second) * per_channel(scale_two)
    padded_grad = extended(grad_second, (("row", 2), ("col", 3)), 1)
    grad_first = (
        spatial_back(padded_grad, w_spatial, height, breadth)
        * silu_grad(first)
        * per_channel(scale_one)
    )
    down_grad = grad_joined + pointwise_back(grad_first, w_reduce)
    expand_term = jnp.einsum("nmhw,nchw->mc", hidden_two, grad_third, precision=highest)
    spatial_term = spatial_weight(padded_one, grad_second, height, breadth)
    reduce_term = jnp.einsum("nchw,nmhw->cm", inputs, grad_first, precision=highest)
    return down_grad, (reduce_term, spatial_term, expand_term)


def gathered_weights(weights, sections):
    flat = jnp.concatenate([w[0].reshape(-1) for w in weights])
    packed = jnp.broadcast_to(flat.reshape(1, -1, 128), (sections, flat.size // 128, 128))
    every = lax.all_to_all(packed, "section", 0, 0, tiled=True).reshape(sections, -1)
    offset, unpacked = (0, [])
    for w in weights:
        size = w[0].size
        unpacked.append(every[:, offset : offset + size].reshape((sections,) + w.shape[1:]))
        offset += size
    return tuple(unpacked)


def reduced_terms(terms, sections):
    shapes = [t.shape for t in terms[0]]
    flat = jnp.stack([jnp.concatenate([t.reshape(-1) for t in ts]) for ts in terms])
    flat = flat.reshape(sections, -1, 128)
    by_image = lax.all_to_all(flat, "section", 0, 0, tiled=True).sum(axis=0)
    group = lax.axis_size("row") * lax.axis_size("col")
    pieces = by_image.reshape(group, -1, 128)
    mine = lax.all_to_all(pieces, ("row", "col"), 0, 0, tiled=True).sum(axis=0)
    copies = jnp.broadcast_to(mine[None], (group,) + mine.shape)
    total = lax.all_to_all(copies, ("row", "col"), 0, 0, tiled=True).reshape(-1)
    out, offset = ([], 0)
    for shape in shapes:
        size = 1
        for d in shape:
            size *= d
        out.append(total[offset : offset + size].reshape(shape))
        offset += size
    return out


def per_device(
    block_input,
    grad_out,
    w_reduce,
    w_spatial,
    w_expand,
    scale_one,
    shift_one,
    scale_two,
    shift_two,
    scale_three,
    shift_three,
):
    sections = lax.axis_size("section")
    me = lax.axis_index("section")
    images = block_input.shape[1]
    mine = lax.all_to_all(block_input[0], "section", 0, 0, tiled=True)
    gathered = gathered_weights(
        (w_reduce, w_spatial, w_expand, scale_one, shift_one, scale_two, shift_two, scale_three, shift_three),
        sections,
    )
    per_image = images // sections
    upstream = lax.dynamic_slice_in_dim(grad_out, me * per_image, per_image, axis=0)
    cells = images * mine.shape[2] * mine.shape[3] * lax.axis_size("row") * lax.axis_size("col")
    factor = 1.0 / jnp.sqrt(jnp.float32(cells))
    saved_all = forward(mine, gathered)
    down = [None] * sections
    terms = [None] * sections
    for sec in range(sections - 1, -1, -1):
        part = slice(sec * per_image, (sec + 1) * per_image)
        weights = tuple(g[sec] for g in gathered)
        saved = tuple(v[part] for v in saved_all)
        upstream, terms[sec] = backward(mine[part], upstream, saved, weights)
        down[sec] = upstream
    results = lax.all_to_all(jnp.concatenate(down, axis=0), "section", 0, 0, tiled=True)
    sums = reduced_terms(terms, sections)
    return (results[None],) + tuple((t * factor)[None] for t in sums)


def solution(mesh):
    placed = (
        P("section", None, None, "row", "col"),
        P(None, None, "row", "col"),
        P("section", None, None),
        P("section", None, None, None, None),
        P("section", None, None),
        P("section", None),
        P("section", None),
        P("section", None),
        P("section", None),
        P("section", None),
        P("section", None),
    )
    return jax.shard_map(
        per_device,
        mesh=mesh,
        in_specs=placed,
        out_specs=(
            P("section", None, None, "row", "col"),
            P("section", None, None),
            P("section", None, None, None, None),
            P("section", None, None),
        ),
        check_vma=False,
    )
```

```python
import jax
import jax.numpy as jnp
from jax import lax
from jax.sharding import PartitionSpec as P

highest = lax.Precision.HIGHEST


def extended(value, sides, width):
    for axis, dim in sides:
        size, length = (lax.axis_size(axis), value.shape[dim])
        up = [(i, (i + 1) % size) for i in range(size - 1)]
        down = [(j, i) for i, j in up]
        last = lax.slice_in_dim(value, length - width, length, axis=dim)
        leading = lax.slice_in_dim(value, 0, width, axis=dim)
        before = lax.ppermute(last, axis, up)
        after = lax.ppermute(leading, axis, down)
        value = jnp.concatenate([before, value, after], axis=dim)
    return value


def silu_grad(values):
    sig = jax.nn.sigmoid(values)
    return sig * (1.0 + values * (1.0 - sig))


def pointwise(values, weight):
    return jnp.einsum("nchw,cm->nmhw", values, weight, precision=highest)


def pointwise_back(values, weight):
    return jnp.einsum("nmhw,cm->nchw", values, weight, precision=highest)


def spatial(padded, weight, height, breadth):
    total = jnp.zeros((padded.shape[0], weight.shape[3], height, breadth), jnp.float32)
    for offset_row in range(3):
        for offset_col in range(3):
            piece = padded[
                :, :, offset_row : offset_row + height, offset_col : offset_col + breadth
            ]
            total = total + pointwise(piece, weight[offset_row, offset_col])
    return total


def spatial_back(padded, weight, height, breadth):
    total = jnp.zeros((padded.shape[0], weight.shape[2], height, breadth), jnp.float32)
    for offset_row in range(3):
        for offset_col in range(3):
            piece = padded[
                :,
                :,
                2 - offset_row : 2 - offset_row + height,
                2 - offset_col : 2 - offset_col + breadth,
            ]
            total = total + pointwise_back(piece, weight[offset_row, offset_col])
    return total


def spatial_weight(padded, grad_second, height, breadth):
    rows_out = []
    for offset_row in range(3):
        cols_out = []
        for offset_col in range(3):
            piece = padded[
                :, :, offset_row : offset_row + height, offset_col : offset_col + breadth
            ]
            cols_out.append(jnp.einsum("nchw,nohw->co", piece, grad_second, precision=highest))
        rows_out.append(jnp.stack(cols_out))
    return jnp.stack(rows_out)


def per_channel(values):
    return values[:, None, None]


def stacked_channel(values):
    return values[:, :, None, None]


def forward(inputs, weights):
    w_reduce, w_spatial, w_expand, scale_one, shift_one, scale_two, shift_two, scale_three, shift_three = weights
    height, breadth = (inputs.shape[2], inputs.shape[3])
    first = jnp.einsum("nchw,ncm->nmhw", inputs, w_reduce, precision=highest)
    first = first * stacked_channel(scale_one) + stacked_channel(shift_one)
    hidden_one = jax.nn.silu(first)
    padded_one = extended(hidden_one, (("row", 2), ("col", 3)), 1)
    second = jnp.zeros((inputs.shape[0], w_spatial.shape[4], height, breadth), jnp.float32)
    for offset_row in range(3):
        for offset_col in range(3):
            piece = padded_one[
                :, :, offset_row : offset_row + height, offset_col : offset_col + breadth
            ]
            second = second + jnp.einsum(
                "nchw,ncm->nmhw", piece, w_spatial[:, offset_row, offset_col], precision=highest
            )
    second = second * stacked_channel(scale_two) + stacked_channel(shift_two)
    hidden_two = jax.nn.silu(second)
    third = jnp.einsum("nchw,ncm->nmhw", hidden_two, w_expand, precision=highest)
    third = third * stacked_channel(scale_three) + stacked_channel(shift_three)
    joined = inputs + third
    return (first, padded_one, second, hidden_two, joined)


def backward(inputs, upstream, saved, weights):
    w_reduce, w_spatial, w_expand, scale_one, shift_one, scale_two, shift_two, scale_three, shift_three = weights
    first, padded_one, second, hidden_two, joined = saved
    height, breadth = (inputs.shape[2], inputs.shape[3])
    grad_joined = upstream * silu_grad(joined)
    grad_third = grad_joined * per_channel(scale_three)
    grad_second = pointwise_back(grad_third, w_expand) * silu_grad(second) * per_channel(scale_two)
    padded_grad = extended(grad_second, (("row", 2), ("col", 3)), 1)
    grad_first = (
        spatial_back(padded_grad, w_spatial, height, breadth)
        * silu_grad(first)
        * per_channel(scale_one)
    )
    down_grad = grad_joined + pointwise_back(grad_first, w_reduce)
    expand_term = jnp.einsum("nmhw,nchw->mc", hidden_two, grad_third, precision=highest)
    spatial_term = spatial_weight(padded_one, grad_second, height, breadth)
    reduce_term = jnp.einsum("nchw,nmhw->cm", inputs, grad_first, precision=highest)
    return down_grad, (reduce_term, spatial_term, expand_term)


def gathered_weights(weights, sections):
    flat = jnp.concatenate([w[0].reshape(-1) for w in weights])
    packed = jnp.broadcast_to(flat.reshape(1, -1, 128), (sections, flat.size // 128, 128))
    every = lax.all_to_all(packed, "section", 0, 0, tiled=True).reshape(sections, -1)
    offset, unpacked = (0, [])
    for w in weights:
        size = w[0].size
        unpacked.append(every[:, offset : offset + size].reshape((sections,) + w.shape[1:]))
        offset += size
    return tuple(unpacked)


def shifted_pieces(stacked, me, sections):
    pieces = [lax.dynamic_index_in_dim(stacked, me, axis=0, keepdims=False)]
    for d in range(1, sections):
        send = lax.dynamic_index_in_dim(stacked, (me + d) % sections, axis=0, keepdims=False)
        pairs = [(k, (k + d) % sections) for k in range(sections)]
        pieces.append(lax.ppermute(send, "section", pairs))
    return pieces


def reduced_terms(terms, me, sections):
    shapes = [t.shape for t in terms[0]]
    flat = jnp.stack([jnp.concatenate([t.reshape(-1) for t in ts]) for ts in terms])
    flat = flat.reshape(sections, -1, 128)
    by_image = sum(shifted_pieces(flat, me, sections))
    group = lax.axis_size("row") * lax.axis_size("col")
    pieces = by_image.reshape(group, -1, 128)
    mine = lax.all_to_all(pieces, ("row", "col"), 0, 0, tiled=True).sum(axis=0)
    copies = jnp.broadcast_to(mine[None], (group,) + mine.shape)
    total = lax.all_to_all(copies, ("row", "col"), 0, 0, tiled=True).reshape(-1)
    out, offset = ([], 0)
    for shape in shapes:
        size = 1
        for d in shape:
            size *= d
        out.append(total[offset : offset + size].reshape(shape))
        offset += size
    return out


def per_device(
    block_input,
    grad_out,
    w_reduce,
    w_spatial,
    w_expand,
    scale_one,
    shift_one,
    scale_two,
    shift_two,
    scale_three,
    shift_three,
):
    sections = lax.axis_size("section")
    me = lax.axis_index("section")
    images = block_input.shape[1]
    mine = lax.all_to_all(block_input[0], "section", 0, 0, tiled=True)
    gathered = gathered_weights(
        (w_reduce, w_spatial, w_expand, scale_one, shift_one, scale_two, shift_two, scale_three, shift_three),
        sections,
    )
    per_image = images // sections
    upstream = lax.dynamic_slice_in_dim(grad_out, me * per_image, per_image, axis=0)
    cells = images * mine.shape[2] * mine.shape[3] * lax.axis_size("row") * lax.axis_size("col")
    factor = 1.0 / jnp.sqrt(jnp.float32(cells))
    saved_all = forward(mine, gathered)
    down = [None] * sections
    terms = [None] * sections
    for sec in range(sections - 1, -1, -1):
        part = slice(sec * per_image, (sec + 1) * per_image)
        weights = tuple(g[sec] for g in gathered)
        saved = tuple(v[part] for v in saved_all)
        upstream, terms[sec] = backward(mine[part], upstream, saved, weights)
        down[sec] = upstream
    pieces = jnp.stack(shifted_pieces(jnp.stack(down), me, sections))
    order = (me - jnp.arange(sections)) % sections
    results = jnp.take(pieces, order, axis=0).reshape((images,) + mine.shape[1:])
    sums = reduced_terms(terms, me, sections)
    return (results[None],) + tuple((t * factor)[None] for t in sums)


def solution(mesh):
    placed = (
        P("section", None, None, "row", "col"),
        P(None, None, "row", "col"),
        P("section", None, None),
        P("section", None, None, None, None),
        P("section", None, None),
        P("section", None),
        P("section", None),
        P("section", None),
        P("section", None),
        P("section", None),
        P("section", None),
    )
    return jax.shard_map(
        per_device,
        mesh=mesh,
        in_specs=placed,
        out_specs=(
            P("section", None, None, "row", "col"),
            P("section", None, None),
            P("section", None, None, None, None),
            P("section", None, None),
        ),
        check_vma=False,
    )
```

```python
import jax
import jax.numpy as jnp
from jax import lax
from jax.sharding import PartitionSpec as P

highest = lax.Precision.HIGHEST


def extended(value, sides, width):
    for axis, dim in sides:
        size, length = (lax.axis_size(axis), value.shape[dim])
        up = [(i, (i + 1) % size) for i in range(size - 1)]
        down = [(j, i) for i, j in up]
        last = lax.slice_in_dim(value, length - width, length, axis=dim)
        leading = lax.slice_in_dim(value, 0, width, axis=dim)
        before = lax.ppermute(last, axis, up)
        after = lax.ppermute(leading, axis, down)
        value = jnp.concatenate([before, value, after], axis=dim)
    return value


def silu_grad(values):
    sig = jax.nn.sigmoid(values)
    return sig * (1.0 + values * (1.0 - sig))


def pointwise(values, weight):
    return jnp.einsum("nchw,cm->nmhw", values, weight, precision=highest)


def pointwise_back(values, weight):
    return jnp.einsum("nmhw,cm->nchw", values, weight, precision=highest)


def taps(padded, height, breadth, flipped):
    pieces = []
    for offset_row in range(3):
        for offset_col in range(3):
            a, b = ((2 - offset_row, 2 - offset_col) if flipped else (offset_row, offset_col))
            pieces.append(padded[:, :, a : a + height, b : b + breadth])
    return jnp.stack(pieces, axis=1)


def spatial_back(padded, weight, height, breadth):
    stacked = taps(padded, height, breadth, True)
    kernel = weight.reshape((9,) + weight.shape[2:])
    return jnp.einsum("nkohw,kco->nchw", stacked, kernel, precision=highest)


def spatial_weight(padded, grad_second, height, breadth):
    stacked = taps(padded, height, breadth, False)
    out = jnp.einsum("nkchw,nohw->kco", stacked, grad_second, precision=highest)
    return out.reshape((3, 3) + out.shape[1:])


def per_channel(values):
    return values[:, None, None]


def stacked_channel(values):
    return values[:, :, None, None]


def forward(inputs, weights):
    w_reduce, w_spatial, w_expand, scale_one, shift_one, scale_two, shift_two, scale_three, shift_three = weights
    height, breadth = (inputs.shape[2], inputs.shape[3])
    first = jnp.einsum("nchw,ncm->nmhw", inputs, w_reduce, precision=highest)
    first = first * stacked_channel(scale_one) + stacked_channel(shift_one)
    hidden_one = jax.nn.silu(first)
    padded_one = extended(hidden_one, (("row", 2), ("col", 3)), 1)
    kernel = w_spatial.reshape((w_spatial.shape[0], 9) + w_spatial.shape[3:])
    second = jnp.einsum(
        "nkchw,nkcm->nmhw", taps(padded_one, height, breadth, False), kernel, precision=highest
    )
    second = second * stacked_channel(scale_two) + stacked_channel(shift_two)
    hidden_two = jax.nn.silu(second)
    third = jnp.einsum("nchw,ncm->nmhw", hidden_two, w_expand, precision=highest)
    third = third * stacked_channel(scale_three) + stacked_channel(shift_three)
    joined = inputs + third
    return (first, padded_one, second, hidden_two, joined)


def backward(inputs, upstream, saved, weights):
    w_reduce, w_spatial, w_expand, scale_one, shift_one, scale_two, shift_two, scale_three, shift_three = weights
    first, padded_one, second, hidden_two, joined = saved
    height, breadth = (inputs.shape[2], inputs.shape[3])
    grad_joined = upstream * silu_grad(joined)
    grad_third = grad_joined * per_channel(scale_three)
    grad_second = pointwise_back(grad_third, w_expand) * silu_grad(second) * per_channel(scale_two)
    padded_grad = extended(grad_second, (("row", 2), ("col", 3)), 1)
    grad_first = (
        spatial_back(padded_grad, w_spatial, height, breadth)
        * silu_grad(first)
        * per_channel(scale_one)
    )
    down_grad = grad_joined + pointwise_back(grad_first, w_reduce)
    expand_term = jnp.einsum("nmhw,nchw->mc", hidden_two, grad_third, precision=highest)
    spatial_term = spatial_weight(padded_one, grad_second, height, breadth)
    reduce_term = jnp.einsum("nchw,nmhw->cm", inputs, grad_first, precision=highest)
    return down_grad, (reduce_term, spatial_term, expand_term)


def gathered_weights(weights, sections):
    flat = jnp.concatenate([w[0].reshape(-1) for w in weights])
    packed = jnp.broadcast_to(flat.reshape(1, -1, 128), (sections, flat.size // 128, 128))
    every = lax.all_to_all(packed, "section", 0, 0, tiled=True).reshape(sections, -1)
    offset, unpacked = (0, [])
    for w in weights:
        size = w[0].size
        unpacked.append(every[:, offset : offset + size].reshape((sections,) + w.shape[1:]))
        offset += size
    return tuple(unpacked)


def shifted_pieces(stacked, me, sections):
    pieces = [lax.dynamic_index_in_dim(stacked, me, axis=0, keepdims=False)]
    for d in range(1, sections):
        send = lax.dynamic_index_in_dim(stacked, (me + d) % sections, axis=0, keepdims=False)
        pairs = [(k, (k + d) % sections) for k in range(sections)]
        pieces.append(lax.ppermute(send, "section", pairs))
    return pieces


def reduced_terms(terms, me, sections):
    shapes = [t.shape for t in terms[0]]
    flat = jnp.stack([jnp.concatenate([t.reshape(-1) for t in ts]) for ts in terms])
    flat = flat.reshape(sections, -1, 128)
    by_image = sum(shifted_pieces(flat, me, sections))
    group = lax.axis_size("row") * lax.axis_size("col")
    pieces = by_image.reshape(group, -1, 128)
    mine = lax.all_to_all(pieces, ("row", "col"), 0, 0, tiled=True).sum(axis=0)
    copies = jnp.broadcast_to(mine[None], (group,) + mine.shape)
    total = lax.all_to_all(copies, ("row", "col"), 0, 0, tiled=True).reshape(-1)
    out, offset = ([], 0)
    for shape in shapes:
        size = 1
        for d in shape:
            size *= d
        out.append(total[offset : offset + size].reshape(shape))
        offset += size
    return out


def per_device(
    block_input,
    grad_out,
    w_reduce,
    w_spatial,
    w_expand,
    scale_one,
    shift_one,
    scale_two,
    shift_two,
    scale_three,
    shift_three,
):
    sections = lax.axis_size("section")
    me = lax.axis_index("section")
    images = block_input.shape[1]
    mine = lax.all_to_all(block_input[0], "section", 0, 0, tiled=True)
    gathered = gathered_weights(
        (w_reduce, w_spatial, w_expand, scale_one, shift_one, scale_two, shift_two, scale_three, shift_three),
        sections,
    )
    per_image = images // sections
    upstream = lax.dynamic_slice_in_dim(grad_out, me * per_image, per_image, axis=0)
    cells = images * mine.shape[2] * mine.shape[3] * lax.axis_size("row") * lax.axis_size("col")
    factor = 1.0 / jnp.sqrt(jnp.float32(cells))
    saved_all = forward(mine, gathered)
    down = [None] * sections
    terms = [None] * sections
    for sec in range(sections - 1, -1, -1):
        part = slice(sec * per_image, (sec + 1) * per_image)
        weights = tuple(g[sec] for g in gathered)
        saved = tuple(v[part] for v in saved_all)
        upstream, terms[sec] = backward(mine[part], upstream, saved, weights)
        down[sec] = upstream
    pieces = jnp.stack(shifted_pieces(jnp.stack(down), me, sections))
    order = (me - jnp.arange(sections)) % sections
    results = jnp.take(pieces, order, axis=0).reshape((images,) + mine.shape[1:])
    sums = reduced_terms(terms, me, sections)
    return (results[None],) + tuple((t * factor)[None] for t in sums)


def solution(mesh):
    placed = (
        P("section", None, None, "row", "col"),
        P(None, None, "row", "col"),
        P("section", None, None),
        P("section", None, None, None, None),
        P("section", None, None),
        P("section", None),
        P("section", None),
        P("section", None),
        P("section", None),
        P("section", None),
        P("section", None),
    )
    return jax.shard_map(
        per_device,
        mesh=mesh,
        in_specs=placed,
        out_specs=(
            P("section", None, None, "row", "col"),
            P("section", None, None),
            P("section", None, None, None, None),
            P("section", None, None),
        ),
        check_vma=False,
    )
```

```python
import jax
import jax.numpy as jnp
from jax import lax
from jax.sharding import PartitionSpec as P

highest = lax.Precision.HIGHEST


def extended(value, sides, width):
    for axis, dim in sides:
        size, length = (lax.axis_size(axis), value.shape[dim])
        up = [(i, (i + 1) % size) for i in range(size - 1)]
        down = [(j, i) for i, j in up]
        last = lax.slice_in_dim(value, length - width, length, axis=dim)
        leading = lax.slice_in_dim(value, 0, width, axis=dim)
        before = lax.ppermute(last, axis, up)
        after = lax.ppermute(leading, axis, down)
        value = jnp.concatenate([before, value, after], axis=dim)
    return value


def silu_grad(values):
    sig = jax.nn.sigmoid(values)
    return sig * (1.0 + values * (1.0 - sig))


def pointwise(values, weight):
    return jnp.einsum("nchw,cm->nmhw", values, weight, precision=highest)


def pointwise_back(values, weight):
    return jnp.einsum("nmhw,cm->nchw", values, weight, precision=highest)


def taps(padded, height, breadth, flipped):
    pieces = []
    for offset_row in range(3):
        for offset_col in range(3):
            a, b = ((2 - offset_row, 2 - offset_col) if flipped else (offset_row, offset_col))
            pieces.append(padded[:, :, a : a + height, b : b + breadth])
    return jnp.stack(pieces, axis=1)


def spatial_back(padded, weight, height, breadth):
    stacked = taps(padded, height, breadth, True)
    kernel = weight.reshape((9,) + weight.shape[2:])
    return jnp.einsum("nkohw,kco->nchw", stacked, kernel, precision=highest)


def spatial_weight(padded, grad_second, height, breadth):
    stacked = taps(padded, height, breadth, False)
    out = jnp.einsum("nkchw,nohw->kco", stacked, grad_second, precision=highest)
    return out.reshape((3, 3) + out.shape[1:])


def per_channel(values):
    return values[:, None, None]


def stacked_channel(values):
    return values[:, :, None, None]


def forward(inputs, weights):
    w_reduce, w_spatial, w_expand, scale_one, shift_one, scale_two, shift_two, scale_three, shift_three = weights
    height, breadth = (inputs.shape[2], inputs.shape[3])
    first = jnp.einsum("nchw,ncm->nmhw", inputs, w_reduce, precision=highest)
    first = first * stacked_channel(scale_one) + stacked_channel(shift_one)
    hidden_one = jax.nn.silu(first)
    padded_one = extended(hidden_one, (("row", 2), ("col", 3)), 1)
    kernel = w_spatial.reshape((w_spatial.shape[0], 9) + w_spatial.shape[3:])
    second = jnp.einsum(
        "nkchw,nkcm->nmhw", taps(padded_one, height, breadth, False), kernel, precision=highest
    )
    second = second * stacked_channel(scale_two) + stacked_channel(shift_two)
    hidden_two = jax.nn.silu(second)
    third = jnp.einsum("nchw,ncm->nmhw", hidden_two, w_expand, precision=highest)
    third = third * stacked_channel(scale_three) + stacked_channel(shift_three)
    joined = inputs + third
    return (first, padded_one, second, hidden_two, joined)


def backward(inputs, upstream, saved, weights):
    w_reduce, w_spatial, w_expand, scale_one, shift_one, scale_two, shift_two, scale_three, shift_three = weights
    first, padded_one, second, hidden_two, joined = saved
    height, breadth = (inputs.shape[2], inputs.shape[3])
    grad_joined = upstream * silu_grad(joined)
    grad_third = grad_joined * per_channel(scale_three)
    grad_second = pointwise_back(grad_third, w_expand) * silu_grad(second) * per_channel(scale_two)
    padded_grad = extended(grad_second, (("row", 2), ("col", 3)), 1)
    grad_first = (
        spatial_back(padded_grad, w_spatial, height, breadth)
        * silu_grad(first)
        * per_channel(scale_one)
    )
    down_grad = grad_joined + pointwise_back(grad_first, w_reduce)
    expand_term = jnp.einsum("nmhw,nchw->mc", hidden_two, grad_third, precision=highest)
    spatial_term = spatial_weight(padded_one, grad_second, height, breadth)
    reduce_term = jnp.einsum("nchw,nmhw->cm", inputs, grad_first, precision=highest)
    return down_grad, (reduce_term, spatial_term, expand_term)


def redistributed(block_input, weights, sections):
    local = block_input[0]
    flat = jnp.concatenate([w[0].reshape(-1) for w in weights]).reshape(1, -1, 128)
    lanes = local.reshape(local.shape[0], -1, 128)
    packed = jnp.concatenate(
        [lanes, jnp.broadcast_to(flat, (sections,) + flat.shape[1:])], axis=1
    )
    every = lax.all_to_all(packed, "section", 0, 0, tiled=True)
    mine = every[:, : lanes.shape[1]].reshape(local.shape)
    every = every[:, lanes.shape[1] :].reshape(sections, -1)
    offset, unpacked = (0, [])
    for w in weights:
        size = w[0].size
        unpacked.append(every[:, offset : offset + size].reshape((sections,) + w.shape[1:]))
        offset += size
    return mine, tuple(unpacked)


def shifted_pieces(stacked, me, sections):
    pieces = [lax.dynamic_index_in_dim(stacked, me, axis=0, keepdims=False)]
    for d in range(1, sections):
        send = lax.dynamic_index_in_dim(stacked, (me + d) % sections, axis=0, keepdims=False)
        pairs = [(k, (k + d) % sections) for k in range(sections)]
        pieces.append(lax.ppermute(send, "section", pairs))
    return pieces


def reduced_terms(terms, me, sections):
    shapes = [t.shape for t in terms[0]]
    flat = jnp.stack([jnp.concatenate([t.reshape(-1) for t in ts]) for ts in terms])
    flat = flat.reshape(sections, -1, 128)
    by_image = sum(shifted_pieces(flat, me, sections))
    group = lax.axis_size("row") * lax.axis_size("col")
    pieces = by_image.reshape(group, -1, 128)
    mine = lax.all_to_all(pieces, ("row", "col"), 0, 0, tiled=True).sum(axis=0)
    copies = jnp.broadcast_to(mine[None], (group,) + mine.shape)
    total = lax.all_to_all(copies, ("row", "col"), 0, 0, tiled=True).reshape(-1)
    out, offset = ([], 0)
    for shape in shapes:
        size = 1
        for d in shape:
            size *= d
        out.append(total[offset : offset + size].reshape(shape))
        offset += size
    return out


def per_device(
    block_input,
    grad_out,
    w_reduce,
    w_spatial,
    w_expand,
    scale_one,
    shift_one,
    scale_two,
    shift_two,
    scale_three,
    shift_three,
):
    sections = lax.axis_size("section")
    me = lax.axis_index("section")
    images = block_input.shape[1]
    mine, gathered = redistributed(
        block_input,
        (w_reduce, w_spatial, w_expand, scale_one, shift_one, scale_two, shift_two, scale_three, shift_three),
        sections,
    )
    per_image = images // sections
    upstream = lax.dynamic_slice_in_dim(grad_out, me * per_image, per_image, axis=0)
    cells = images * mine.shape[2] * mine.shape[3] * lax.axis_size("row") * lax.axis_size("col")
    factor = 1.0 / jnp.sqrt(jnp.float32(cells))
    saved_all = forward(mine, gathered)
    down = [None] * sections
    terms = [None] * sections
    for sec in range(sections - 1, -1, -1):
        part = slice(sec * per_image, (sec + 1) * per_image)
        weights = tuple(g[sec] for g in gathered)
        saved = tuple(v[part] for v in saved_all)
        upstream, terms[sec] = backward(mine[part], upstream, saved, weights)
        down[sec] = upstream
    pieces = jnp.stack(shifted_pieces(jnp.stack(down), me, sections))
    order = (me - jnp.arange(sections)) % sections
    results = jnp.take(pieces, order, axis=0).reshape((images,) + mine.shape[1:])
    sums = reduced_terms(terms, me, sections)
    return (results[None],) + tuple((t * factor)[None] for t in sums)


def solution(mesh):
    placed = (
        P("section", None, None, "row", "col"),
        P(None, None, "row", "col"),
        P("section", None, None),
        P("section", None, None, None, None),
        P("section", None, None),
        P("section", None),
        P("section", None),
        P("section", None),
        P("section", None),
        P("section", None),
        P("section", None),
    )
    return jax.shard_map(
        per_device,
        mesh=mesh,
        in_specs=placed,
        out_specs=(
            P("section", None, None, "row", "col"),
            P("section", None, None),
            P("section", None, None, None, None),
            P("section", None, None),
        ),
        check_vma=False,
    )
```

```python
import jax
import jax.numpy as jnp
from jax import lax
from jax.sharding import PartitionSpec as P

highest = lax.Precision.HIGHEST


def extended(value, sides, width):
    for axis, dim in sides:
        size, length = (lax.axis_size(axis), value.shape[dim])
        up = [(i, (i + 1) % size) for i in range(size - 1)]
        down = [(j, i) for i, j in up]
        last = lax.slice_in_dim(value, length - width, length, axis=dim)
        leading = lax.slice_in_dim(value, 0, width, axis=dim)
        before = lax.ppermute(last, axis, up)
        after = lax.ppermute(leading, axis, down)
        value = jnp.concatenate([before, value, after], axis=dim)
    return value


def silu_grad(values):
    sig = jax.nn.sigmoid(values)
    return sig * (1.0 + values * (1.0 - sig))


def pointwise(values, weight):
    return jnp.einsum("nchw,cm->nmhw", values, weight, precision=highest)


def pointwise_back(values, weight):
    return jnp.einsum("nmhw,cm->nchw", values, weight, precision=highest)


def taps(padded, height, breadth, flipped):
    pieces = []
    for offset_row in range(3):
        for offset_col in range(3):
            a, b = ((2 - offset_row, 2 - offset_col) if flipped else (offset_row, offset_col))
            pieces.append(padded[:, :, a : a + height, b : b + breadth])
    return jnp.stack(pieces, axis=1)


def spatial_back(padded, weight, height, breadth):
    stacked = taps(padded, height, breadth, True)
    kernel = weight.reshape((9,) + weight.shape[2:])
    return jnp.einsum("nkohw,kco->nchw", stacked, kernel, precision=highest)


def spatial_weight(padded, grad_second, height, breadth):
    stacked = taps(padded, height, breadth, False)
    out = jnp.einsum("nkchw,nohw->kco", stacked, grad_second, precision=highest)
    return out.reshape((3, 3) + out.shape[1:])


def per_channel(values):
    return values[:, None, None]


def stacked_channel(values):
    return values[:, :, None, None]


def forward(inputs, weights):
    w_reduce, w_spatial, w_expand, scale_one, shift_one, scale_two, shift_two, scale_three, shift_three = weights
    height, breadth = (inputs.shape[2], inputs.shape[3])
    first = jnp.einsum("nchw,ncm->nmhw", inputs, w_reduce, precision=highest)
    first = first * stacked_channel(scale_one) + stacked_channel(shift_one)
    hidden_one = jax.nn.silu(first)
    padded_one = extended(hidden_one, (("row", 2), ("col", 3)), 1)
    kernel = w_spatial.reshape((w_spatial.shape[0], 9) + w_spatial.shape[3:])
    second = jnp.einsum(
        "nkchw,nkcm->nmhw", taps(padded_one, height, breadth, False), kernel, precision=highest
    )
    second = second * stacked_channel(scale_two) + stacked_channel(shift_two)
    hidden_two = jax.nn.silu(second)
    third = jnp.einsum("nmhw,ncm->nchw", hidden_two, w_expand, precision=highest)
    third = third * stacked_channel(scale_three) + stacked_channel(shift_three)
    joined = inputs + third
    return (first, padded_one, second, hidden_two, joined)


def backward(inputs, upstream, saved, weights):
    w_reduce, w_spatial, w_expand, scale_one, shift_one, scale_two, shift_two, scale_three, shift_three = weights
    first, padded_one, second, hidden_two, joined = saved
    height, breadth = (inputs.shape[2], inputs.shape[3])
    grad_joined = upstream * silu_grad(joined)
    grad_third = grad_joined * per_channel(scale_three)
    grad_second = pointwise(grad_third, w_expand) * silu_grad(second) * per_channel(scale_two)
    padded_grad = extended(grad_second, (("row", 2), ("col", 3)), 1)
    grad_first = (
        spatial_back(padded_grad, w_spatial, height, breadth)
        * silu_grad(first)
        * per_channel(scale_one)
    )
    down_grad = grad_joined + pointwise_back(grad_first, w_reduce)
    expand_term = jnp.einsum("nmhw,nchw->mc", hidden_two, grad_third, precision=highest)
    spatial_term = spatial_weight(padded_one, grad_second, height, breadth)
    reduce_term = jnp.einsum("nchw,nmhw->cm", inputs, grad_first, precision=highest)
    return down_grad, (reduce_term, spatial_term, expand_term)


def gathered_weights(weights, sections):
    w_reduce, w_spatial, w_expand, scale_one, shift_one, scale_two, shift_two, scale_three, shift_three = (
        w[0] for w in weights
    )
    lanes = w_reduce.shape[1]
    rows = [
        w_reduce,
        w_spatial.reshape(-1, lanes),
        w_expand.T,
        jnp.stack([scale_one, shift_one, scale_two, shift_two]),
        scale_three.reshape(-1, lanes),
        shift_three.reshape(-1, lanes),
    ]
    flat = jnp.concatenate(rows)
    packed = jnp.broadcast_to(flat[None], (sections,) + flat.shape)
    every = lax.all_to_all(packed, "section", 0, 0, tiled=True)
    parts, offset = ([], 0)
    for r in rows:
        parts.append(every[:, offset : offset + r.shape[0]])
        offset += r.shape[0]
    small = parts[3]
    return (
        parts[0],
        parts[1].reshape((sections,) + w_spatial.shape),
        parts[2],
        small[:, 0],
        small[:, 1],
        small[:, 2],
        small[:, 3],
        parts[4].reshape(sections, -1),
        parts[5].reshape(sections, -1),
    )


def shifted_pieces(stacked, me, sections):
    pieces = [lax.dynamic_index_in_dim(stacked, me, axis=0, keepdims=False)]
    for d in range(1, sections):
        send = lax.dynamic_index_in_dim(stacked, (me + d) % sections, axis=0, keepdims=False)
        pairs = [(k, (k + d) % sections) for k in range(sections)]
        pieces.append(lax.ppermute(send, "section", pairs))
    return pieces


def reduced_terms(terms, me, sections):
    shapes = [t.shape for t in terms[0]]
    flat = jnp.stack([jnp.concatenate([t.reshape(-1) for t in ts]) for ts in terms])
    flat = flat.reshape(sections, -1, 128)
    by_image = sum(shifted_pieces(flat, me, sections))
    group = lax.axis_size("row") * lax.axis_size("col")
    pieces = by_image.reshape(group, -1, 128)
    mine = lax.all_to_all(pieces, ("row", "col"), 0, 0, tiled=True).sum(axis=0)
    copies = jnp.broadcast_to(mine[None], (group,) + mine.shape)
    total = lax.all_to_all(copies, ("row", "col"), 0, 0, tiled=True).reshape(-1)
    out, offset = ([], 0)
    for shape in shapes:
        size = 1
        for d in shape:
            size *= d
        out.append(total[offset : offset + size].reshape(shape))
        offset += size
    return out


def per_device(
    block_input,
    grad_out,
    w_reduce,
    w_spatial,
    w_expand,
    scale_one,
    shift_one,
    scale_two,
    shift_two,
    scale_three,
    shift_three,
):
    sections = lax.axis_size("section")
    me = lax.axis_index("section")
    images = block_input.shape[1]
    mine = lax.all_to_all(block_input[0], "section", 0, 0, tiled=True)
    gathered = gathered_weights(
        (w_reduce, w_spatial, w_expand, scale_one, shift_one, scale_two, shift_two, scale_three, shift_three),
        sections,
    )
    per_image = images // sections
    upstream = lax.dynamic_slice_in_dim(grad_out, me * per_image, per_image, axis=0)
    cells = images * mine.shape[2] * mine.shape[3] * lax.axis_size("row") * lax.axis_size("col")
    factor = 1.0 / jnp.sqrt(jnp.float32(cells))
    saved_all = forward(mine, gathered)
    down = [None] * sections
    terms = [None] * sections
    for sec in range(sections - 1, -1, -1):
        part = slice(sec * per_image, (sec + 1) * per_image)
        weights = tuple(g[sec] for g in gathered)
        saved = tuple(v[part] for v in saved_all)
        upstream, terms[sec] = backward(mine[part], upstream, saved, weights)
        down[sec] = upstream
    pieces = jnp.stack(shifted_pieces(jnp.stack(down), me, sections))
    order = (me - jnp.arange(sections)) % sections
    results = jnp.take(pieces, order, axis=0).reshape((images,) + mine.shape[1:])
    sums = reduced_terms(terms, me, sections)
    return (results[None],) + tuple((t * factor)[None] for t in sums)


def solution(mesh):
    placed = (
        P("section", None, None, "row", "col"),
        P(None, None, "row", "col"),
        P("section", None, None),
        P("section", None, None, None, None),
        P("section", None, None),
        P("section", None),
        P("section", None),
        P("section", None),
        P("section", None),
        P("section", None),
        P("section", None),
    )
    return jax.shard_map(
        per_device,
        mesh=mesh,
        in_specs=placed,
        out_specs=(
            P("section", None, None, "row", "col"),
            P("section", None, None),
            P("section", None, None, None, None),
            P("section", None, None),
        ),
        check_vma=False,
    )
```

```python
import jax
import jax.numpy as jnp
from jax import lax
from jax.sharding import PartitionSpec as P

highest = lax.Precision.HIGHEST


def extended(value, sides, width):
    for axis, dim in sides:
        size, length = (lax.axis_size(axis), value.shape[dim])
        up = [(i, (i + 1) % size) for i in range(size - 1)]
        down = [(j, i) for i, j in up]
        last = lax.slice_in_dim(value, length - width, length, axis=dim)
        leading = lax.slice_in_dim(value, 0, width, axis=dim)
        before = lax.ppermute(last, axis, up)
        after = lax.ppermute(leading, axis, down)
        value = jnp.concatenate([before, value, after], axis=dim)
    return value


def silu_grad(values):
    sig = jax.nn.sigmoid(values)
    return sig * (1.0 + values * (1.0 - sig))


def pointwise(values, weight):
    return jnp.einsum("nchw,cm->nmhw", values, weight, precision=highest)


def pointwise_back(values, weight):
    return jnp.einsum("nmhw,cm->nchw", values, weight, precision=highest)


def taps(padded, height, breadth, flipped):
    pieces = []
    for offset_row in range(3):
        for offset_col in range(3):
            a, b = ((2 - offset_row, 2 - offset_col) if flipped else (offset_row, offset_col))
            pieces.append(padded[:, :, a : a + height, b : b + breadth])
    return jnp.stack(pieces, axis=1)


def spatial_back(padded, weight, height, breadth):
    stacked = taps(padded, height, breadth, True)
    kernel = weight.reshape((9,) + weight.shape[2:])
    return jnp.einsum("nkohw,kco->nchw", stacked, kernel, precision=highest)


def spatial_weight(padded, grad_second, height, breadth):
    stacked = taps(padded, height, breadth, False)
    out = jnp.einsum("nkchw,nohw->kco", stacked, grad_second, precision=highest)
    return out.reshape((3, 3) + out.shape[1:])


def per_channel(values):
    return values[:, None, None]


def stacked_channel(values):
    return values[:, :, None, None]


def forward(inputs, weights):
    w_reduce, w_spatial, w_expand, scale_one, shift_one, scale_two, shift_two, scale_three, shift_three = weights
    height, breadth = (inputs.shape[2], inputs.shape[3])
    first = jnp.einsum("nchw,ncm->nmhw", inputs, w_reduce, precision=highest)
    first = first * stacked_channel(scale_one) + stacked_channel(shift_one)
    hidden_one = jax.nn.silu(first)
    padded_one = extended(hidden_one, (("row", 2), ("col", 3)), 1)
    kernel = w_spatial.reshape((w_spatial.shape[0], 9) + w_spatial.shape[3:])
    second = jnp.einsum(
        "nkchw,nkcm->nmhw", taps(padded_one, height, breadth, False), kernel, precision=highest
    )
    second = second * stacked_channel(scale_two) + stacked_channel(shift_two)
    hidden_two = jax.nn.silu(second)
    third = jnp.einsum("nmhw,ncm->nchw", hidden_two, w_expand, precision=highest)
    third = third * stacked_channel(scale_three) + stacked_channel(shift_three)
    joined = inputs + third
    return (first, padded_one, second, hidden_two, joined)


def backward(inputs, upstream, saved, weights):
    w_reduce, w_spatial, w_expand, scale_one, shift_one, scale_two, shift_two, scale_three, shift_three = weights
    first, padded_one, second, hidden_two, joined = saved
    height, breadth = (inputs.shape[2], inputs.shape[3])
    grad_joined = upstream * silu_grad(joined)
    grad_third = grad_joined * per_channel(scale_three)
    grad_second = pointwise(grad_third, w_expand) * silu_grad(second) * per_channel(scale_two)
    padded_grad = extended(grad_second, (("row", 2), ("col", 3)), 1)
    grad_first = (
        spatial_back(padded_grad, w_spatial, height, breadth)
        * silu_grad(first)
        * per_channel(scale_one)
    )
    down_grad = grad_joined + pointwise_back(grad_first, w_reduce)
    expand_term = jnp.einsum("nmhw,nchw->mc", hidden_two, grad_third, precision=highest)
    spatial_term = spatial_weight(padded_one, grad_second, height, breadth)
    reduce_term = jnp.einsum("nchw,nmhw->cm", inputs, grad_first, precision=highest)
    return down_grad, (reduce_term, spatial_term, expand_term)


def spread(value, pick, sections):
    me = lax.axis_index("section")
    pieces = [value[me] if pick else value]
    for d in range(1, sections):
        send = value[(me + d) % sections] if pick else value
        pairs = [(k, (k + d) % sections) for k in range(sections)]
        pieces.append(lax.ppermute(send, "section", pairs))
    order = (me - jnp.arange(sections)) % sections
    return jnp.take(jnp.stack(pieces), order, axis=0)


def gathered_weights(weights, sections):
    w_reduce, w_spatial, w_expand, scale_one, shift_one, scale_two, shift_two, scale_three, shift_three = (
        w[0] for w in weights
    )
    lanes = w_reduce.shape[1]
    rows = [
        w_reduce,
        w_spatial.reshape(-1, lanes),
        w_expand.T,
        jnp.stack([scale_one, shift_one, scale_two, shift_two]),
        scale_three.reshape(-1, lanes),
        shift_three.reshape(-1, lanes),
    ]
    flat = jnp.concatenate(rows)
    every = spread(flat, None, sections)
    parts, offset = ([], 0)
    for r in rows:
        parts.append(every[:, offset : offset + r.shape[0]])
        offset += r.shape[0]
    small = parts[3]
    return (
        parts[0],
        parts[1].reshape((sections,) + w_spatial.shape),
        parts[2],
        small[:, 0],
        small[:, 1],
        small[:, 2],
        small[:, 3],
        parts[4].reshape(sections, -1),
        parts[5].reshape(sections, -1),
    )


def shifted_pieces(stacked, me, sections):
    pieces = [lax.dynamic_index_in_dim(stacked, me, axis=0, keepdims=False)]
    for d in range(1, sections):
        send = lax.dynamic_index_in_dim(stacked, (me + d) % sections, axis=0, keepdims=False)
        pairs = [(k, (k + d) % sections) for k in range(sections)]
        pieces.append(lax.ppermute(send, "section", pairs))
    return pieces


def reduced_terms(terms, me, sections):
    shapes = [t.shape for t in terms[0]]
    flat = jnp.stack([jnp.concatenate([t.reshape(-1) for t in ts]) for ts in terms])
    flat = flat.reshape(sections, -1, 128)
    by_image = sum(shifted_pieces(flat, me, sections))
    group = lax.axis_size("row") * lax.axis_size("col")
    pieces = by_image.reshape(group, -1, 128)
    mine = lax.all_to_all(pieces, ("row", "col"), 0, 0, tiled=True).sum(axis=0)
    copies = jnp.broadcast_to(mine[None], (group,) + mine.shape)
    total = lax.all_to_all(copies, ("row", "col"), 0, 0, tiled=True).reshape(-1)
    out, offset = ([], 0)
    for shape in shapes:
        size = 1
        for d in shape:
            size *= d
        out.append(total[offset : offset + size].reshape(shape))
        offset += size
    return out


def per_device(
    block_input,
    grad_out,
    w_reduce,
    w_spatial,
    w_expand,
    scale_one,
    shift_one,
    scale_two,
    shift_two,
    scale_three,
    shift_three,
):
    sections = lax.axis_size("section")
    me = lax.axis_index("section")
    images = block_input.shape[1]
    mine = spread(block_input[0], True, sections)
    gathered = gathered_weights(
        (w_reduce, w_spatial, w_expand, scale_one, shift_one, scale_two, shift_two, scale_three, shift_three),
        sections,
    )
    per_image = images // sections
    upstream = lax.dynamic_slice_in_dim(grad_out, me * per_image, per_image, axis=0)
    cells = images * mine.shape[2] * mine.shape[3] * lax.axis_size("row") * lax.axis_size("col")
    factor = 1.0 / jnp.sqrt(jnp.float32(cells))
    saved_all = forward(mine, gathered)
    down = [None] * sections
    terms = [None] * sections
    for sec in range(sections - 1, -1, -1):
        part = slice(sec * per_image, (sec + 1) * per_image)
        weights = tuple(g[sec] for g in gathered)
        saved = tuple(v[part] for v in saved_all)
        upstream, terms[sec] = backward(mine[part], upstream, saved, weights)
        down[sec] = upstream
    pieces = jnp.stack(shifted_pieces(jnp.stack(down), me, sections))
    order = (me - jnp.arange(sections)) % sections
    results = jnp.take(pieces, order, axis=0).reshape((images,) + mine.shape[1:])
    sums = reduced_terms(terms, me, sections)
    return (results[None],) + tuple((t * factor)[None] for t in sums)


def solution(mesh):
    placed = (
        P("section", None, None, "row", "col"),
        P(None, None, "row", "col"),
        P("section", None, None),
        P("section", None, None, None, None),
        P("section", None, None),
        P("section", None),
        P("section", None),
        P("section", None),
        P("section", None),
        P("section", None),
        P("section", None),
    )
    return jax.shard_map(
        per_device,
        mesh=mesh,
        in_specs=placed,
        out_specs=(
            P("section", None, None, "row", "col"),
            P("section", None, None),
            P("section", None, None, None, None),
            P("section", None, None),
        ),
        check_vma=False,
    )
```

```python
import jax
import jax.numpy as jnp
from jax import lax
from jax.sharding import PartitionSpec as P

highest = lax.Precision.HIGHEST


def extended(value, sides, width):
    for axis, dim in sides:
        size, length = (lax.axis_size(axis), value.shape[dim])
        up = [(i, (i + 1) % size) for i in range(size - 1)]
        down = [(j, i) for i, j in up]
        last = lax.slice_in_dim(value, length - width, length, axis=dim)
        leading = lax.slice_in_dim(value, 0, width, axis=dim)
        before = lax.ppermute(last, axis, up)
        after = lax.ppermute(leading, axis, down)
        value = jnp.concatenate([before, value, after], axis=dim)
    return value


def silu_grad(values):
    sig = jax.nn.sigmoid(values)
    return sig * (1.0 + values * (1.0 - sig))


def pointwise(values, weight):
    return jnp.einsum("nchw,cm->nmhw", values, weight, precision=highest)


def pointwise_back(values, weight):
    return jnp.einsum("nmhw,cm->nchw", values, weight, precision=highest)


def taps(padded, height, breadth, flipped):
    pieces = []
    for offset_row in range(3):
        for offset_col in range(3):
            a, b = ((2 - offset_row, 2 - offset_col) if flipped else (offset_row, offset_col))
            pieces.append(padded[:, :, a : a + height, b : b + breadth])
    return jnp.stack(pieces, axis=1)


def spatial_back(padded, weight, height, breadth):
    stacked = taps(padded, height, breadth, True)
    kernel = weight.reshape((9,) + weight.shape[2:])
    return jnp.einsum("nkohw,kco->nchw", stacked, kernel, precision=highest)


def spatial_weight(padded, grad_second, height, breadth):
    stacked = taps(padded, height, breadth, False)
    out = jnp.einsum("nkchw,nohw->kco", stacked, grad_second, precision=highest)
    return out.reshape((3, 3) + out.shape[1:])


def per_channel(values):
    return values[:, None, None]


def stacked_channel(values):
    return values[:, :, None, None]


def forward(inputs, weights):
    w_reduce, w_spatial, w_expand, scale_one, shift_one, scale_two, shift_two, scale_three, shift_three = weights
    height, breadth = (inputs.shape[2], inputs.shape[3])
    first = jnp.einsum("nchw,ncm->nmhw", inputs, w_reduce, precision=highest)
    first = first * stacked_channel(scale_one) + stacked_channel(shift_one)
    hidden_one = jax.nn.silu(first)
    padded_one = extended(hidden_one, (("row", 2), ("col", 3)), 1)
    kernel = w_spatial.reshape((w_spatial.shape[0], 9) + w_spatial.shape[3:])
    second = jnp.einsum(
        "nkchw,nkcm->nmhw", taps(padded_one, height, breadth, False), kernel, precision=highest
    )
    second = second * stacked_channel(scale_two) + stacked_channel(shift_two)
    hidden_two = jax.nn.silu(second)
    third = jnp.einsum("nmhw,ncm->nchw", hidden_two, w_expand, precision=highest)
    third = third * stacked_channel(scale_three) + stacked_channel(shift_three)
    joined = inputs + third
    return (first, padded_one, second, hidden_two, joined)


def backward(inputs, upstream, saved, weights):
    w_reduce, w_spatial, w_expand, scale_one, shift_one, scale_two, shift_two, scale_three, shift_three = weights
    first, padded_one, second, hidden_two, joined = saved
    height, breadth = (inputs.shape[2], inputs.shape[3])
    grad_joined = upstream * silu_grad(joined)
    grad_third = grad_joined * per_channel(scale_three)
    grad_second = pointwise(grad_third, w_expand) * silu_grad(second) * per_channel(scale_two)
    padded_grad = extended(grad_second, (("row", 2), ("col", 3)), 1)
    grad_first = (
        spatial_back(padded_grad, w_spatial, height, breadth)
        * silu_grad(first)
        * per_channel(scale_one)
    )
    down_grad = grad_joined + pointwise_back(grad_first, w_reduce)
    expand_term = jnp.einsum("nmhw,nchw->mc", hidden_two, grad_third, precision=highest)
    spatial_term = spatial_weight(padded_one, grad_second, height, breadth)
    reduce_term = jnp.einsum("nchw,nmhw->cm", inputs, grad_first, precision=highest)
    return down_grad, (reduce_term, spatial_term, expand_term)


def gathered_weights(weights, sections):
    w_reduce, w_spatial, w_expand, scale_one, shift_one, scale_two, shift_two, scale_three, shift_three = (
        w[0] for w in weights
    )
    lanes = w_reduce.shape[1]
    rows = [
        w_reduce,
        w_spatial.reshape(-1, lanes),
        w_expand.T,
        jnp.stack([scale_one, shift_one, scale_two, shift_two]),
        scale_three.reshape(-1, lanes),
        shift_three.reshape(-1, lanes),
    ]
    flat = jnp.concatenate(rows)
    packed = jnp.broadcast_to(flat[None], (sections,) + flat.shape)
    every = lax.all_to_all(packed, "section", 0, 0, tiled=True)
    parts, offset = ([], 0)
    for r in rows:
        parts.append(every[:, offset : offset + r.shape[0]])
        offset += r.shape[0]
    small = parts[3]
    return (
        parts[0],
        parts[1].reshape((sections,) + w_spatial.shape),
        parts[2],
        small[:, 0],
        small[:, 1],
        small[:, 2],
        small[:, 3],
        parts[4].reshape(sections, -1),
        parts[5].reshape(sections, -1),
    )


def shifted_pieces(stacked, me, sections):
    pieces = [lax.dynamic_index_in_dim(stacked, me, axis=0, keepdims=False)]
    for d in range(1, sections):
        send = lax.dynamic_index_in_dim(stacked, (me + d) % sections, axis=0, keepdims=False)
        pairs = [(k, (k + d) % sections) for k in range(sections)]
        pieces.append(lax.ppermute(send, "section", pairs))
    return pieces


def reduced_terms(terms, me, sections):
    shapes = [t.shape for t in terms[0]]
    flat = jnp.stack([jnp.concatenate([t.reshape(-1) for t in ts]) for ts in terms])
    group = lax.axis_size("row") * lax.axis_size("col")
    pieces = flat.reshape(sections, group, -1, 128).transpose(1, 0, 2, 3)
    scattered = lax.all_to_all(pieces, ("row", "col"), 0, 0, tiled=True).sum(axis=0)
    mine = sum(shifted_pieces(scattered, me, sections))
    copies = jnp.broadcast_to(mine[None], (group,) + mine.shape)
    total = lax.all_to_all(copies, ("row", "col"), 0, 0, tiled=True).reshape(-1)
    out, offset = ([], 0)
    for shape in shapes:
        size = 1
        for d in shape:
            size *= d
        out.append(total[offset : offset + size].reshape(shape))
        offset += size
    return out


def per_device(
    block_input,
    grad_out,
    w_reduce,
    w_spatial,
    w_expand,
    scale_one,
    shift_one,
    scale_two,
    shift_two,
    scale_three,
    shift_three,
):
    sections = lax.axis_size("section")
    me = lax.axis_index("section")
    images = block_input.shape[1]
    mine = lax.all_to_all(block_input[0], "section", 0, 0, tiled=True)
    gathered = gathered_weights(
        (w_reduce, w_spatial, w_expand, scale_one, shift_one, scale_two, shift_two, scale_three, shift_three),
        sections,
    )
    per_image = images // sections
    upstream = lax.dynamic_slice_in_dim(grad_out, me * per_image, per_image, axis=0)
    cells = images * mine.shape[2] * mine.shape[3] * lax.axis_size("row") * lax.axis_size("col")
    factor = 1.0 / jnp.sqrt(jnp.float32(cells))
    saved_all = forward(mine, gathered)
    down = [None] * sections
    terms = [None] * sections
    for sec in range(sections - 1, -1, -1):
        part = slice(sec * per_image, (sec + 1) * per_image)
        weights = tuple(g[sec] for g in gathered)
        saved = tuple(v[part] for v in saved_all)
        upstream, terms[sec] = backward(mine[part], upstream, saved, weights)
        down[sec] = upstream
    pieces = jnp.stack(shifted_pieces(jnp.stack(down), me, sections))
    order = (me - jnp.arange(sections)) % sections
    results = jnp.take(pieces, order, axis=0).reshape((images,) + mine.shape[1:])
    sums = reduced_terms(terms, me, sections)
    return (results[None],) + tuple((t * factor)[None] for t in sums)


def solution(mesh):
    placed = (
        P("section", None, None, "row", "col"),
        P(None, None, "row", "col"),
        P("section", None, None),
        P("section", None, None, None, None),
        P("section", None, None),
        P("section", None),
        P("section", None),
        P("section", None),
        P("section", None),
        P("section", None),
        P("section", None),
    )
    return jax.shard_map(
        per_device,
        mesh=mesh,
        in_specs=placed,
        out_specs=(
            P("section", None, None, "row", "col"),
            P("section", None, None),
            P("section", None, None, None, None),
            P("section", None, None),
        ),
        check_vma=False,
    )
```

```python
import jax
import jax.numpy as jnp
from jax import lax
from jax.sharding import PartitionSpec as P

highest = lax.Precision.HIGHEST


def extended(value, sides, width):
    for axis, dim in sides:
        size, length = (lax.axis_size(axis), value.shape[dim])
        up = [(i, (i + 1) % size) for i in range(size - 1)]
        down = [(j, i) for i, j in up]
        last = lax.slice_in_dim(value, length - width, length, axis=dim)
        leading = lax.slice_in_dim(value, 0, width, axis=dim)
        before = lax.ppermute(last, axis, up)
        after = lax.ppermute(leading, axis, down)
        value = jnp.concatenate([before, value, after], axis=dim)
    return value


def silu_grad(values):
    sig = jax.nn.sigmoid(values)
    return sig * (1.0 + values * (1.0 - sig))


def pointwise(values, weight):
    return jnp.einsum("nchw,cm->nmhw", values, weight, precision=highest)


def pointwise_back(values, weight):
    return jnp.einsum("nmhw,cm->nchw", values, weight, precision=highest)


def taps(padded, height, breadth, flipped):
    pieces = []
    for offset_row in range(3):
        for offset_col in range(3):
            a, b = ((2 - offset_row, 2 - offset_col) if flipped else (offset_row, offset_col))
            pieces.append(padded[:, :, a : a + height, b : b + breadth])
    return jnp.stack(pieces, axis=1)


def spatial_back(padded, weight, height, breadth):
    stacked = taps(padded, height, breadth, True)
    kernel = weight.reshape((9,) + weight.shape[2:])
    return jnp.einsum("nkohw,kco->nchw", stacked, kernel, precision=highest)


def spatial_weight(padded, grad_second, height, breadth):
    stacked = taps(padded, height, breadth, False)
    out = jnp.einsum("nkchw,nohw->kco", stacked, grad_second, precision=highest)
    return out.reshape((3, 3) + out.shape[1:])


def per_channel(values):
    return values[:, None, None]


def stacked_channel(values):
    return values[:, :, None, None]


def forward(inputs, weights):
    w_reduce, w_spatial, w_expand, scale_one, shift_one, scale_two, shift_two, scale_three, shift_three = weights
    height, breadth = (inputs.shape[2], inputs.shape[3])
    first = jnp.einsum("nchw,ncm->nmhw", inputs, w_reduce, precision=highest)
    first = first * stacked_channel(scale_one) + stacked_channel(shift_one)
    hidden_one = jax.nn.silu(first)
    padded_one = extended(hidden_one, (("row", 2), ("col", 3)), 1)
    kernel = w_spatial.reshape((w_spatial.shape[0], 9) + w_spatial.shape[3:])
    second = jnp.einsum(
        "nkchw,nkcm->nmhw", taps(padded_one, height, breadth, False), kernel, precision=highest
    )
    second = second * stacked_channel(scale_two) + stacked_channel(shift_two)
    hidden_two = jax.nn.silu(second)
    third = jnp.einsum("nmhw,ncm->nchw", hidden_two, w_expand, precision=highest)
    third = third * stacked_channel(scale_three) + stacked_channel(shift_three)
    joined = inputs + third
    return (first, padded_one, second, hidden_two, joined)


def backward(inputs, upstream, saved, weights):
    w_reduce, w_spatial, w_expand, scale_one, shift_one, scale_two, shift_two, scale_three, shift_three = weights
    first, padded_one, second, hidden_two, joined = saved
    height, breadth = (inputs.shape[2], inputs.shape[3])
    grad_joined = upstream * silu_grad(joined)
    grad_third = grad_joined * per_channel(scale_three)
    grad_second = pointwise(grad_third, w_expand) * silu_grad(second) * per_channel(scale_two)
    padded_grad = extended(grad_second, (("row", 2), ("col", 3)), 1)
    grad_first = (
        spatial_back(padded_grad, w_spatial, height, breadth)
        * silu_grad(first)
        * per_channel(scale_one)
    )
    down_grad = grad_joined + pointwise_back(grad_first, w_reduce)
    return down_grad, (grad_third, grad_second, grad_first)


def weight_terms(inputs, saved, grads):
    first, padded_one, second, hidden_two, joined = saved
    grad_third, grad_second, grad_first = grads
    height, breadth = (inputs.shape[2], inputs.shape[3])
    expand_term = jnp.einsum("nmhw,nchw->nmc", hidden_two, grad_third, precision=highest)
    stacked = taps(padded_one, height, breadth, False)
    spatial_term = jnp.einsum("nkchw,nohw->nkco", stacked, grad_second, precision=highest)
    reduce_term = jnp.einsum("nchw,nmhw->ncm", inputs, grad_first, precision=highest)
    sections = inputs.shape[0]
    flat = jnp.concatenate(
        [t.reshape(sections, -1) for t in (reduce_term, spatial_term, expand_term)], axis=1
    )
    shapes = [reduce_term.shape[1:], (3, 3) + spatial_term.shape[2:], expand_term.shape[1:]]
    return flat, shapes


def gathered_weights(weights, sections):
    w_reduce, w_spatial, w_expand, scale_one, shift_one, scale_two, shift_two, scale_three, shift_three = (
        w[0] for w in weights
    )
    lanes = w_reduce.shape[1]
    rows = [
        w_reduce,
        w_spatial.reshape(-1, lanes),
        w_expand.T,
        jnp.stack([scale_one, shift_one, scale_two, shift_two]),
        scale_three.reshape(-1, lanes),
        shift_three.reshape(-1, lanes),
    ]
    flat = jnp.concatenate(rows)
    packed = jnp.broadcast_to(flat[None], (sections,) + flat.shape)
    every = lax.all_to_all(packed, "section", 0, 0, tiled=True)
    parts, offset = ([], 0)
    for r in rows:
        parts.append(every[:, offset : offset + r.shape[0]])
        offset += r.shape[0]
    small = parts[3]
    return (
        parts[0],
        parts[1].reshape((sections,) + w_spatial.shape),
        parts[2],
        small[:, 0],
        small[:, 1],
        small[:, 2],
        small[:, 3],
        parts[4].reshape(sections, -1),
        parts[5].reshape(sections, -1),
    )


def shifted_pieces(stacked, me, sections):
    pieces = [lax.dynamic_index_in_dim(stacked, me, axis=0, keepdims=False)]
    for d in range(1, sections):
        send = lax.dynamic_index_in_dim(stacked, (me + d) % sections, axis=0, keepdims=False)
        pairs = [(k, (k + d) % sections) for k in range(sections)]
        pieces.append(lax.ppermute(send, "section", pairs))
    return pieces


def reduced_terms(flat, shapes, me, sections):
    flat = flat.reshape(sections, -1, 128)
    by_image = sum(shifted_pieces(flat, me, sections))
    group = lax.axis_size("row") * lax.axis_size("col")
    pieces = by_image.reshape(group, -1, 128)
    mine = lax.all_to_all(pieces, ("row", "col"), 0, 0, tiled=True).sum(axis=0)
    copies = jnp.broadcast_to(mine[None], (group,) + mine.shape)
    total = lax.all_to_all(copies, ("row", "col"), 0, 0, tiled=True).reshape(-1)
    out, offset = ([], 0)
    for shape in shapes:
        size = 1
        for d in shape:
            size *= d
        out.append(total[offset : offset + size].reshape(shape))
        offset += size
    return out


def per_device(
    block_input,
    grad_out,
    w_reduce,
    w_spatial,
    w_expand,
    scale_one,
    shift_one,
    scale_two,
    shift_two,
    scale_three,
    shift_three,
):
    sections = lax.axis_size("section")
    me = lax.axis_index("section")
    images = block_input.shape[1]
    mine = lax.all_to_all(block_input[0], "section", 0, 0, tiled=True)
    gathered = gathered_weights(
        (w_reduce, w_spatial, w_expand, scale_one, shift_one, scale_two, shift_two, scale_three, shift_three),
        sections,
    )
    per_image = images // sections
    upstream = lax.dynamic_slice_in_dim(grad_out, me * per_image, per_image, axis=0)
    cells = images * mine.shape[2] * mine.shape[3] * lax.axis_size("row") * lax.axis_size("col")
    factor = 1.0 / jnp.sqrt(jnp.float32(cells))
    saved_all = forward(mine, gathered)
    down = [None] * sections
    grads = [None] * sections
    for sec in range(sections - 1, -1, -1):
        part = slice(sec * per_image, (sec + 1) * per_image)
        weights = tuple(g[sec] for g in gathered)
        saved = tuple(v[part] for v in saved_all)
        upstream, grads[sec] = backward(mine[part], upstream, saved, weights)
        down[sec] = upstream
    pieces = jnp.stack(shifted_pieces(jnp.stack(down), me, sections))
    order = (me - jnp.arange(sections)) % sections
    results = jnp.take(pieces, order, axis=0).reshape((images,) + mine.shape[1:])
    stacked_grads = tuple(jnp.concatenate([g[k] for g in grads]) for k in range(3))
    flat, shapes = weight_terms(mine, saved_all, stacked_grads)
    sums = reduced_terms(flat, shapes, me, sections)
    return (results[None],) + tuple((t * factor)[None] for t in sums)


def solution(mesh):
    placed = (
        P("section", None, None, "row", "col"),
        P(None, None, "row", "col"),
        P("section", None, None),
        P("section", None, None, None, None),
        P("section", None, None),
        P("section", None),
        P("section", None),
        P("section", None),
        P("section", None),
        P("section", None),
        P("section", None),
    )
    return jax.shard_map(
        per_device,
        mesh=mesh,
        in_specs=placed,
        out_specs=(
            P("section", None, None, "row", "col"),
            P("section", None, None),
            P("section", None, None, None, None),
            P("section", None, None),
        ),
        check_vma=False,
    )
```

```python
import jax
import jax.numpy as jnp
from jax import lax
from jax.sharding import PartitionSpec as P

highest = lax.Precision.HIGHEST


def extended(value, sides, width):
    for axis, dim in sides:
        size, length = (lax.axis_size(axis), value.shape[dim])
        up = [(i, (i + 1) % size) for i in range(size - 1)]
        down = [(j, i) for i, j in up]
        last = lax.slice_in_dim(value, length - width, length, axis=dim)
        leading = lax.slice_in_dim(value, 0, width, axis=dim)
        before = lax.ppermute(last, axis, up)
        after = lax.ppermute(leading, axis, down)
        value = jnp.concatenate([before, value, after], axis=dim)
    return value


def silu_grad(values):
    sig = jax.nn.sigmoid(values)
    return sig * (1.0 + values * (1.0 - sig))


def pointwise(values, weight):
    return jnp.einsum("nchw,cm->nmhw", values, weight, precision=highest)


def pointwise_back(values, weight):
    return jnp.einsum("nmhw,cm->nchw", values, weight, precision=highest)


def taps(padded, height, breadth, flipped):
    pieces = []
    for offset_row in range(3):
        for offset_col in range(3):
            a, b = ((2 - offset_row, 2 - offset_col) if flipped else (offset_row, offset_col))
            pieces.append(padded[:, :, a : a + height, b : b + breadth])
    return jnp.stack(pieces, axis=1)


def spatial_back(padded, weight, height, breadth):
    stacked = taps(padded, height, breadth, True)
    kernel = weight.reshape((9,) + weight.shape[2:])
    return jnp.einsum("nkohw,kco->nchw", stacked, kernel, precision=highest)


def spatial_weight(padded, grad_second, height, breadth):
    stacked = taps(padded, height, breadth, False)
    out = jnp.einsum("nkchw,nohw->kco", stacked, grad_second, precision=highest)
    return out.reshape((3, 3) + out.shape[1:])


def per_channel(values):
    return values[:, None, None]


def stacked_channel(values):
    return values[:, :, None, None]


def forward(inputs, weights):
    w_reduce, w_spatial, w_expand, scale_one, shift_one, scale_two, shift_two, scale_three, shift_three = weights
    height, breadth = (inputs.shape[2], inputs.shape[3])
    first = jnp.einsum("nchw,ncm->nmhw", inputs, w_reduce, precision=highest)
    first = first * stacked_channel(scale_one) + stacked_channel(shift_one)
    hidden_one = jax.nn.silu(first)
    padded_one = extended(hidden_one, (("row", 2), ("col", 3)), 1)
    kernel = w_spatial.reshape((w_spatial.shape[0], 9) + w_spatial.shape[3:])
    second = jnp.einsum(
        "nkchw,nkcm->nmhw", taps(padded_one, height, breadth, False), kernel, precision=highest
    )
    second = second * stacked_channel(scale_two) + stacked_channel(shift_two)
    hidden_two = jax.nn.silu(second)
    third = jnp.einsum("nmhw,ncm->nchw", hidden_two, w_expand, precision=highest)
    third = third * stacked_channel(scale_three) + stacked_channel(shift_three)
    joined = inputs + third
    return (first, padded_one, second, hidden_two, joined)


def backward(inputs, upstream, saved, weights):
    w_reduce, w_spatial, w_expand, scale_one, shift_one, scale_two, shift_two, scale_three, shift_three = weights
    first, padded_one, second, hidden_two, joined = saved
    height, breadth = (inputs.shape[2], inputs.shape[3])
    grad_joined = upstream * silu_grad(joined)
    grad_third = grad_joined * per_channel(scale_three)
    grad_second = pointwise(grad_third, w_expand) * silu_grad(second) * per_channel(scale_two)
    padded_grad = extended(grad_second, (("row", 2), ("col", 3)), 1)
    grad_first = (
        spatial_back(padded_grad, w_spatial, height, breadth)
        * silu_grad(first)
        * per_channel(scale_one)
    )
    down_grad = grad_joined + pointwise_back(grad_first, w_reduce)
    return down_grad, (grad_third, grad_second, grad_first)


def weight_terms(inputs, saved, grads):
    first, padded_one, second, hidden_two, joined = saved
    grad_third, grad_second, grad_first = grads
    height, breadth = (inputs.shape[2], inputs.shape[3])
    expand_term = jnp.einsum("nmhw,nchw->nmc", hidden_two, grad_third, precision=highest)
    stacked = taps(padded_one, height, breadth, False)
    spatial_term = jnp.einsum("nkchw,nohw->nkco", stacked, grad_second, precision=highest)
    reduce_term = jnp.einsum("nchw,nmhw->ncm", inputs, grad_first, precision=highest)
    sections = inputs.shape[0]
    flat = jnp.concatenate(
        [t.reshape(sections, -1) for t in (reduce_term, spatial_term, expand_term)], axis=1
    )
    shapes = [reduce_term.shape[1:], (3, 3) + spatial_term.shape[2:], expand_term.shape[1:]]
    return flat, shapes


def gathered_weights(weights, sections):
    w_reduce, w_spatial, w_expand, scale_one, shift_one, scale_two, shift_two, scale_three, shift_three = (
        w[0] for w in weights
    )
    lanes = w_reduce.shape[1]
    rows = [
        w_reduce,
        w_spatial.reshape(-1, lanes),
        w_expand.T,
        jnp.stack([scale_one, shift_one, scale_two, shift_two]),
        scale_three.reshape(-1, lanes),
        shift_three.reshape(-1, lanes),
    ]
    flat = jnp.concatenate(rows)
    packed = jnp.broadcast_to(flat[None], (sections,) + flat.shape)
    every = lax.all_to_all(packed, "section", 0, 0, tiled=True)
    parts, offset = ([], 0)
    for r in rows:
        parts.append(every[:, offset : offset + r.shape[0]])
        offset += r.shape[0]
    small = parts[3]
    return (
        parts[0],
        parts[1].reshape((sections,) + w_spatial.shape),
        parts[2],
        small[:, 0],
        small[:, 1],
        small[:, 2],
        small[:, 3],
        parts[4].reshape(sections, -1),
        parts[5].reshape(sections, -1),
    )


def shifted_pieces(stacked, me, sections):
    pieces = [lax.dynamic_index_in_dim(stacked, me, axis=0, keepdims=False)]
    for d in range(1, sections):
        send = lax.dynamic_index_in_dim(stacked, (me + d) % sections, axis=0, keepdims=False)
        pairs = [(k, (k + d) % sections) for k in range(sections)]
        pieces.append(lax.ppermute(send, "section", pairs))
    return pieces


def reduced_terms(flat, shapes, me, sections):
    flat = flat.reshape(sections, -1, 128)
    by_image = sum(shifted_pieces(flat, me, sections))
    group = lax.axis_size("row") * lax.axis_size("col")
    pieces = by_image.reshape(group, -1, 128)
    mine = lax.all_to_all(pieces, ("row", "col"), 0, 0, tiled=True).sum(axis=0)
    copies = jnp.broadcast_to(mine[None], (group,) + mine.shape)
    total = lax.all_to_all(copies, ("row", "col"), 0, 0, tiled=True).reshape(-1)
    out, offset = ([], 0)
    for shape in shapes:
        size = 1
        for d in shape:
            size *= d
        out.append(total[offset : offset + size].reshape(shape))
        offset += size
    return out


def per_device(
    block_input,
    grad_out,
    w_reduce,
    w_spatial,
    w_expand,
    scale_one,
    shift_one,
    scale_two,
    shift_two,
    scale_three,
    shift_three,
):
    sections = lax.axis_size("section")
    me = lax.axis_index("section")
    images = block_input.shape[1]
    mine = lax.all_to_all(block_input[0], "section", 0, 0, tiled=True)
    gathered = gathered_weights(
        (w_reduce, w_spatial, w_expand, scale_one, shift_one, scale_two, shift_two, scale_three, shift_three),
        sections,
    )
    per_image = images // sections
    upstream = lax.dynamic_slice_in_dim(grad_out, me * per_image, per_image, axis=0)
    cells = images * mine.shape[2] * mine.shape[3] * lax.axis_size("row") * lax.axis_size("col")
    factor = 1.0 / jnp.sqrt(jnp.float32(cells))
    saved_all = forward(mine, gathered)

    def step(upstream, sec):
        weights = tuple(lax.dynamic_index_in_dim(g, sec, keepdims=False) for g in gathered)
        saved = tuple(lax.dynamic_slice_in_dim(v, sec * per_image, per_image) for v in saved_all)
        inputs = lax.dynamic_slice_in_dim(mine, sec * per_image, per_image)
        down_grad, grads = backward(inputs, upstream, saved, weights)
        return down_grad, (down_grad, grads)

    _, (downs, grads) = lax.scan(step, upstream, jnp.arange(sections - 1, -1, -1))
    down = [downs[sections - 1 - sec] for sec in range(sections)]
    stacked_grads = tuple(
        jnp.concatenate([g[sections - 1 - sec] for sec in range(sections)]) for g in grads
    )
    pieces = jnp.stack(shifted_pieces(jnp.stack(down), me, sections))
    order = (me - jnp.arange(sections)) % sections
    results = jnp.take(pieces, order, axis=0).reshape((images,) + mine.shape[1:])
    flat, shapes = weight_terms(mine, saved_all, stacked_grads)
    sums = reduced_terms(flat, shapes, me, sections)
    return (results[None],) + tuple((t * factor)[None] for t in sums)


def solution(mesh):
    placed = (
        P("section", None, None, "row", "col"),
        P(None, None, "row", "col"),
        P("section", None, None),
        P("section", None, None, None, None),
        P("section", None, None),
        P("section", None),
        P("section", None),
        P("section", None),
        P("section", None),
        P("section", None),
        P("section", None),
    )
    return jax.shard_map(
        per_device,
        mesh=mesh,
        in_specs=placed,
        out_specs=(
            P("section", None, None, "row", "col"),
            P("section", None, None),
            P("section", None, None, None, None),
            P("section", None, None),
        ),
        check_vma=False,
    )
```

```python
import jax
import jax.numpy as jnp
from jax import lax
from jax.sharding import PartitionSpec as P

highest = lax.Precision.HIGHEST


def extended(value, sides, width):
    for axis, dim in sides:
        size, length = (lax.axis_size(axis), value.shape[dim])
        up = [(i, (i + 1) % size) for i in range(size - 1)]
        down = [(j, i) for i, j in up]
        last = lax.slice_in_dim(value, length - width, length, axis=dim)
        leading = lax.slice_in_dim(value, 0, width, axis=dim)
        before = lax.ppermute(last, axis, up)
        after = lax.ppermute(leading, axis, down)
        value = jnp.concatenate([before, value, after], axis=dim)
    return value


def silu_grad(values):
    sig = jax.nn.sigmoid(values)
    return sig * (1.0 + values * (1.0 - sig))


def pointwise(values, weight):
    return jnp.einsum("nchw,cm->nmhw", values, weight, precision=highest)


def pointwise_back(values, weight):
    return jnp.einsum("nmhw,cm->nchw", values, weight, precision=highest)


def taps(padded, height, breadth, flipped):
    pieces = []
    for offset_row in range(3):
        for offset_col in range(3):
            a, b = ((2 - offset_row, 2 - offset_col) if flipped else (offset_row, offset_col))
            pieces.append(padded[:, :, a : a + height, b : b + breadth])
    return jnp.stack(pieces, axis=1)


def spatial_back(padded, weight, height, breadth):
    stacked = taps(padded, height, breadth, True)
    kernel = weight.reshape((9,) + weight.shape[2:])
    return jnp.einsum("nkohw,kco->nchw", stacked, kernel, precision=highest)


def spatial_weight(padded, grad_second, height, breadth):
    stacked = taps(padded, height, breadth, False)
    out = jnp.einsum("nkchw,nohw->kco", stacked, grad_second, precision=highest)
    return out.reshape((3, 3) + out.shape[1:])


def per_channel(values):
    return values[:, None, None]


def stacked_channel(values):
    return values[:, :, None, None]


def forward(inputs, weights):
    w_reduce, w_spatial, w_expand, scale_one, shift_one, scale_two, shift_two, scale_three, shift_three = weights
    height, breadth = (inputs.shape[2], inputs.shape[3])
    first = jnp.einsum("nchw,ncm->nmhw", inputs, w_reduce, precision=highest)
    first = first * stacked_channel(scale_one) + stacked_channel(shift_one)
    hidden_one = jax.nn.silu(first)
    padded_one = extended(hidden_one, (("row", 2), ("col", 3)), 1)
    kernel = w_spatial.reshape((w_spatial.shape[0], 9) + w_spatial.shape[3:])
    second = jnp.einsum(
        "nkchw,nkcm->nmhw", taps(padded_one, height, breadth, False), kernel, precision=highest
    )
    second = second * stacked_channel(scale_two) + stacked_channel(shift_two)
    hidden_two = jax.nn.silu(second)
    third = jnp.einsum("nmhw,ncm->nchw", hidden_two, w_expand, precision=highest)
    third = third * stacked_channel(scale_three) + stacked_channel(shift_three)
    joined = inputs + third
    return (first, padded_one, second, hidden_two, joined)


def backward(inputs, upstream, saved, weights):
    w_reduce, w_spatial, w_expand, scale_one, shift_one, scale_two, shift_two, scale_three, shift_three = weights
    first, padded_one, second, hidden_two, joined = saved
    height, breadth = (inputs.shape[2], inputs.shape[3])
    grad_joined = upstream * silu_grad(joined)
    grad_third = grad_joined * per_channel(scale_three)
    grad_second = pointwise(grad_third, w_expand) * silu_grad(second) * per_channel(scale_two)
    padded_grad = extended(grad_second, (("row", 2), ("col", 3)), 1)
    grad_first = (
        spatial_back(padded_grad, w_spatial, height, breadth)
        * silu_grad(first)
        * per_channel(scale_one)
    )
    down_grad = grad_joined + pointwise_back(grad_first, w_reduce)
    return down_grad, (grad_third, grad_second, grad_first)


def weight_terms(inputs, saved, grads):
    first, padded_one, second, hidden_two, joined = saved
    grad_third, grad_second, grad_first = grads
    height, breadth = (inputs.shape[2], inputs.shape[3])
    expand_term = jnp.einsum("nmhw,nchw->nmc", hidden_two, grad_third, precision=highest)
    stacked = taps(padded_one, height, breadth, False)
    spatial_term = jnp.einsum("nkchw,nohw->nkco", stacked, grad_second, precision=highest)
    reduce_term = jnp.einsum("nchw,nmhw->ncm", inputs, grad_first, precision=highest)
    sections = inputs.shape[0]
    flat = jnp.concatenate(
        [t.reshape(sections, -1) for t in (reduce_term, spatial_term, expand_term)], axis=1
    )
    shapes = [reduce_term.shape[1:], (3, 3) + spatial_term.shape[2:], expand_term.shape[1:]]
    return flat, shapes


def gathered_weights(weights, sections):
    w_reduce, w_spatial, w_expand, scale_one, shift_one, scale_two, shift_two, scale_three, shift_three = (
        w[0] for w in weights
    )
    lanes = w_reduce.shape[1]
    rows = [
        w_reduce,
        w_spatial.reshape(-1, lanes),
        w_expand.T,
        jnp.stack([scale_one, shift_one, scale_two, shift_two]),
        scale_three.reshape(-1, lanes),
        shift_three.reshape(-1, lanes),
    ]
    flat = jnp.concatenate(rows)
    packed = jnp.broadcast_to(flat[None], (sections,) + flat.shape)
    every = lax.all_to_all(packed, "section", 0, 0, tiled=True)
    parts, offset = ([], 0)
    for r in rows:
        parts.append(every[:, offset : offset + r.shape[0]])
        offset += r.shape[0]
    small = parts[3]
    return (
        parts[0],
        parts[1].reshape((sections,) + w_spatial.shape),
        parts[2],
        small[:, 0],
        small[:, 1],
        small[:, 2],
        small[:, 3],
        parts[4].reshape(sections, -1),
        parts[5].reshape(sections, -1),
    )


def shifted_pieces(stacked, me, sections):
    pieces = [lax.dynamic_index_in_dim(stacked, me, axis=0, keepdims=False)]
    for d in range(1, sections):
        send = lax.dynamic_index_in_dim(stacked, (me + d) % sections, axis=0, keepdims=False)
        pairs = [(k, (k + d) % sections) for k in range(sections)]
        pieces.append(lax.ppermute(send, "section", pairs))
    return pieces


def reduced_terms(flat, shapes, me, sections, factor):
    flat = flat.reshape(sections, -1, 128)
    by_image = sum(shifted_pieces(flat, me, sections))
    group = lax.axis_size("row") * lax.axis_size("col")
    pieces = by_image.reshape(group, -1, 128)
    mine = lax.all_to_all(pieces, ("row", "col"), 0, 0, tiled=True).sum(axis=0) * factor
    copies = jnp.broadcast_to(mine[None], (group,) + mine.shape)
    total = lax.all_to_all(copies, ("row", "col"), 0, 0, tiled=True).reshape(-1)
    out, offset = ([], 0)
    for shape in shapes:
        size = 1
        for d in shape:
            size *= d
        out.append(total[offset : offset + size].reshape(shape))
        offset += size
    return out


def per_device(
    block_input,
    grad_out,
    w_reduce,
    w_spatial,
    w_expand,
    scale_one,
    shift_one,
    scale_two,
    shift_two,
    scale_three,
    shift_three,
):
    sections = lax.axis_size("section")
    me = lax.axis_index("section")
    images = block_input.shape[1]
    mine = lax.all_to_all(block_input[0], "section", 0, 0, tiled=True)
    gathered = gathered_weights(
        (w_reduce, w_spatial, w_expand, scale_one, shift_one, scale_two, shift_two, scale_three, shift_three),
        sections,
    )
    per_image = images // sections
    upstream = lax.dynamic_slice_in_dim(grad_out, me * per_image, per_image, axis=0)
    cells = images * mine.shape[2] * mine.shape[3] * lax.axis_size("row") * lax.axis_size("col")
    factor = 1.0 / jnp.sqrt(jnp.float32(cells))
    saved_all = forward(mine, gathered)
    down = [None] * sections
    grads = [None] * sections
    for sec in range(sections - 1, -1, -1):
        part = slice(sec * per_image, (sec + 1) * per_image)
        weights = tuple(g[sec] for g in gathered)
        saved = tuple(v[part] for v in saved_all)
        upstream, grads[sec] = backward(mine[part], upstream, saved, weights)
        down[sec] = upstream
    pieces = jnp.stack(shifted_pieces(jnp.stack(down), me, sections))
    order = (me - jnp.arange(sections)) % sections
    results = jnp.take(pieces, order, axis=0).reshape((images,) + mine.shape[1:])
    stacked_grads = tuple(jnp.concatenate([g[k] for g in grads]) for k in range(3))
    flat, shapes = weight_terms(mine, saved_all, stacked_grads)
    sums = reduced_terms(flat, shapes, me, sections, factor)
    return (results[None],) + tuple(t[None] for t in sums)


def solution(mesh):
    placed = (
        P("section", None, None, "row", "col"),
        P(None, None, "row", "col"),
        P("section", None, None),
        P("section", None, None, None, None),
        P("section", None, None),
        P("section", None),
        P("section", None),
        P("section", None),
        P("section", None),
        P("section", None),
        P("section", None),
    )
    return jax.shard_map(
        per_device,
        mesh=mesh,
        in_specs=placed,
        out_specs=(
            P("section", None, None, "row", "col"),
            P("section", None, None),
            P("section", None, None, None, None),
            P("section", None, None),
        ),
        check_vma=False,
    )
```

```python
import jax
import jax.numpy as jnp
from jax import lax
from jax.sharding import PartitionSpec as P

highest = lax.Precision.HIGHEST


def extended(value, sides, width):
    for axis, dim in sides:
        size, length = (lax.axis_size(axis), value.shape[dim])
        up = [(i, (i + 1) % size) for i in range(size - 1)]
        down = [(j, i) for i, j in up]
        last = lax.slice_in_dim(value, length - width, length, axis=dim)
        leading = lax.slice_in_dim(value, 0, width, axis=dim)
        before = lax.ppermute(last, axis, up)
        after = lax.ppermute(leading, axis, down)
        value = jnp.concatenate([before, value, after], axis=dim)
    return value


def silu_grad(values):
    sig = jax.nn.sigmoid(values)
    return sig * (1.0 + values * (1.0 - sig))


def pointwise(values, weight):
    return jnp.einsum("nchw,cm->nmhw", values, weight, precision=highest)


def pointwise_back(values, weight):
    return jnp.einsum("nmhw,cm->nchw", values, weight, precision=highest)


def taps(padded, height, breadth, flipped):
    pieces = []
    for offset_row in range(3):
        for offset_col in range(3):
            a, b = ((2 - offset_row, 2 - offset_col) if flipped else (offset_row, offset_col))
            pieces.append(padded[:, :, a : a + height, b : b + breadth])
    return jnp.stack(pieces, axis=1)


def spatial_back(padded, weight, height, breadth):
    stacked = taps(padded, height, breadth, True)
    kernel = weight.reshape((9,) + weight.shape[2:])
    return jnp.einsum("nkohw,kco->nchw", stacked, kernel, precision=highest)


def spatial_weight(padded, grad_second, height, breadth):
    stacked = taps(padded, height, breadth, False)
    out = jnp.einsum("nkchw,nohw->kco", stacked, grad_second, precision=highest)
    return out.reshape((3, 3) + out.shape[1:])


def per_channel(values):
    return values[:, None, None]


def stacked_channel(values):
    return values[:, :, None, None]


def forward(inputs, weights):
    w_reduce, w_spatial, w_expand, scale_one, shift_one, scale_two, shift_two, scale_three, shift_three = weights
    height, breadth = (inputs.shape[2], inputs.shape[3])
    first = jnp.einsum("nchw,ncm->nmhw", inputs, w_reduce, precision=highest)
    first = first * stacked_channel(scale_one) + stacked_channel(shift_one)
    hidden_one = jax.nn.silu(first)
    padded_one = extended(hidden_one, (("row", 2), ("col", 3)), 1)
    kernel = w_spatial.reshape((w_spatial.shape[0], 9) + w_spatial.shape[3:])
    second = jnp.einsum(
        "nkchw,nkcm->nmhw", taps(padded_one, height, breadth, False), kernel, precision=highest
    )
    second = second * stacked_channel(scale_two) + stacked_channel(shift_two)
    hidden_two = jax.nn.silu(second)
    third = jnp.einsum("nmhw,ncm->nchw", hidden_two, w_expand, precision=highest)
    third = third * stacked_channel(scale_three) + stacked_channel(shift_three)
    joined = inputs + third
    return (first, padded_one, second, hidden_two, joined)


def backward(inputs, upstream, saved, weights):
    w_reduce, w_spatial, w_expand, scale_one, shift_one, scale_two, shift_two, scale_three, shift_three = weights
    first, padded_one, second, hidden_two, joined = saved
    height, breadth = (inputs.shape[2], inputs.shape[3])
    grad_joined = upstream * silu_grad(joined)
    grad_third = grad_joined * per_channel(scale_three)
    grad_second = pointwise(grad_third, w_expand) * silu_grad(second) * per_channel(scale_two)
    padded_grad = extended(grad_second, (("col", 3), ("row", 2)), 1)
    grad_first = (
        spatial_back(padded_grad, w_spatial, height, breadth)
        * silu_grad(first)
        * per_channel(scale_one)
    )
    down_grad = grad_joined + pointwise_back(grad_first, w_reduce)
    return down_grad, (grad_third, grad_second, grad_first)


def weight_terms(inputs, saved, grads):
    first, padded_one, second, hidden_two, joined = saved
    grad_third, grad_second, grad_first = grads
    height, breadth = (inputs.shape[2], inputs.shape[3])
    expand_term = jnp.einsum("nmhw,nchw->nmc", hidden_two, grad_third, precision=highest)
    stacked = taps(padded_one, height, breadth, False)
    spatial_term = jnp.einsum("nkchw,nohw->nkco", stacked, grad_second, precision=highest)
    reduce_term = jnp.einsum("nchw,nmhw->ncm", inputs, grad_first, precision=highest)
    sections = inputs.shape[0]
    flat = jnp.concatenate(
        [t.reshape(sections, -1) for t in (reduce_term, spatial_term, expand_term)], axis=1
    )
    shapes = [reduce_term.shape[1:], (3, 3) + spatial_term.shape[2:], expand_term.shape[1:]]
    return flat, shapes


def gathered_weights(weights, sections):
    w_reduce, w_spatial, w_expand, scale_one, shift_one, scale_two, shift_two, scale_three, shift_three = (
        w[0] for w in weights
    )
    lanes = w_reduce.shape[1]
    rows = [
        w_reduce,
        w_spatial.reshape(-1, lanes),
        w_expand.T,
        jnp.stack([scale_one, shift_one, scale_two, shift_two]),
        scale_three.reshape(-1, lanes),
        shift_three.reshape(-1, lanes),
    ]
    flat = jnp.concatenate(rows)
    packed = jnp.broadcast_to(flat[None], (sections,) + flat.shape)
    every = lax.all_to_all(packed, "section", 0, 0, tiled=True)
    parts, offset = ([], 0)
    for r in rows:
        parts.append(every[:, offset : offset + r.shape[0]])
        offset += r.shape[0]
    small = parts[3]
    return (
        parts[0],
        parts[1].reshape((sections,) + w_spatial.shape),
        parts[2],
        small[:, 0],
        small[:, 1],
        small[:, 2],
        small[:, 3],
        parts[4].reshape(sections, -1),
        parts[5].reshape(sections, -1),
    )


def shifted_pieces(stacked, me, sections):
    pieces = [lax.dynamic_index_in_dim(stacked, me, axis=0, keepdims=False)]
    for d in range(1, sections):
        send = lax.dynamic_index_in_dim(stacked, (me + d) % sections, axis=0, keepdims=False)
        pairs = [(k, (k + d) % sections) for k in range(sections)]
        pieces.append(lax.ppermute(send, "section", pairs))
    return pieces


def reduced_terms(flat, shapes, me, sections, factor):
    flat = flat.reshape(sections, -1, 128)
    by_image = sum(shifted_pieces(flat, me, sections))
    group = lax.axis_size("row") * lax.axis_size("col")
    pieces = by_image.reshape(group, -1, 128)
    mine = lax.all_to_all(pieces, ("row", "col"), 0, 0, tiled=True).sum(axis=0) * factor
    copies = jnp.broadcast_to(mine[None], (group,) + mine.shape)
    total = lax.all_to_all(copies, ("row", "col"), 0, 0, tiled=True).reshape(-1)
    out, offset = ([], 0)
    for shape in shapes:
        size = 1
        for d in shape:
            size *= d
        out.append(total[offset : offset + size].reshape(shape))
        offset += size
    return out


def per_device(
    block_input,
    grad_out,
    w_reduce,
    w_spatial,
    w_expand,
    scale_one,
    shift_one,
    scale_two,
    shift_two,
    scale_three,
    shift_three,
):
    sections = lax.axis_size("section")
    me = lax.axis_index("section")
    images = block_input.shape[1]
    mine = lax.all_to_all(block_input[0], "section", 0, 0, tiled=True)
    gathered = gathered_weights(
        (w_reduce, w_spatial, w_expand, scale_one, shift_one, scale_two, shift_two, scale_three, shift_three),
        sections,
    )
    per_image = images // sections
    upstream = lax.dynamic_slice_in_dim(grad_out, me * per_image, per_image, axis=0)
    cells = images * mine.shape[2] * mine.shape[3] * lax.axis_size("row") * lax.axis_size("col")
    factor = 1.0 / jnp.sqrt(jnp.float32(cells))
    saved_all = forward(mine, gathered)
    down = [None] * sections
    grads = [None] * sections
    for sec in range(sections - 1, -1, -1):
        part = slice(sec * per_image, (sec + 1) * per_image)
        weights = tuple(g[sec] for g in gathered)
        saved = tuple(v[part] for v in saved_all)
        upstream, grads[sec] = backward(mine[part], upstream, saved, weights)
        down[sec] = upstream
    pieces = jnp.stack(shifted_pieces(jnp.stack(down), me, sections))
    order = (me - jnp.arange(sections)) % sections
    results = jnp.take(pieces, order, axis=0).reshape((images,) + mine.shape[1:])
    stacked_grads = tuple(jnp.concatenate([g[k] for g in grads]) for k in range(3))
    flat, shapes = weight_terms(mine, saved_all, stacked_grads)
    sums = reduced_terms(flat, shapes, me, sections, factor)
    return (results[None],) + tuple(t[None] for t in sums)


def solution(mesh):
    placed = (
        P("section", None, None, "row", "col"),
        P(None, None, "row", "col"),
        P("section", None, None),
        P("section", None, None, None, None),
        P("section", None, None),
        P("section", None),
        P("section", None),
        P("section", None),
        P("section", None),
        P("section", None),
        P("section", None),
    )
    return jax.shard_map(
        per_device,
        mesh=mesh,
        in_specs=placed,
        out_specs=(
            P("section", None, None, "row", "col"),
            P("section", None, None),
            P("section", None, None, None, None),
            P("section", None, None),
        ),
        check_vma=False,
    )
```

```python
import jax
import jax.numpy as jnp
from jax import lax
from jax.sharding import PartitionSpec as P

highest = lax.Precision.HIGHEST


def extended(value, sides, width):
    for axis, dim in sides:
        size, length = (lax.axis_size(axis), value.shape[dim])
        up = [(i, (i + 1) % size) for i in range(size - 1)]
        down = [(j, i) for i, j in up]
        last = lax.slice_in_dim(value, length - width, length, axis=dim)
        leading = lax.slice_in_dim(value, 0, width, axis=dim)
        before = lax.ppermute(last, axis, up)
        after = lax.ppermute(leading, axis, down)
        value = jnp.concatenate([before, value, after], axis=dim)
    return value


def silu_grad(values):
    sig = jax.nn.sigmoid(values)
    return sig * (1.0 + values * (1.0 - sig))


def pointwise(values, weight):
    return jnp.einsum("nchw,cm->nmhw", values, weight, precision=highest)


def pointwise_back(values, weight):
    return jnp.einsum("nmhw,cm->nchw", values, weight, precision=highest)


def taps(padded, height, breadth, flipped):
    pieces = []
    for offset_row in range(3):
        for offset_col in range(3):
            a, b = ((2 - offset_row, 2 - offset_col) if flipped else (offset_row, offset_col))
            pieces.append(padded[:, :, a : a + height, b : b + breadth])
    return jnp.stack(pieces, axis=1)


def spatial_back(padded, weight, height, breadth):
    stacked = taps(padded, height, breadth, True)
    kernel = weight.reshape((9,) + weight.shape[2:])
    return jnp.einsum("nkohw,kco->nchw", stacked, kernel, precision=highest)


def spatial_weight(padded, grad_second, height, breadth):
    stacked = taps(padded, height, breadth, False)
    out = jnp.einsum("nkchw,nohw->kco", stacked, grad_second, precision=highest)
    return out.reshape((3, 3) + out.shape[1:])


def per_channel(values):
    return values[:, None, None]


def stacked_channel(values):
    return values[:, :, None, None]


def forward(inputs, weights):
    w_reduce, w_spatial, w_expand, scale_one, shift_one, scale_two, shift_two, scale_three, shift_three = weights
    height, breadth = (inputs.shape[2], inputs.shape[3])
    first = jnp.einsum("nchw,ncm->nmhw", inputs, w_reduce, precision=highest)
    first = first * stacked_channel(scale_one) + stacked_channel(shift_one)
    hidden_one = jax.nn.silu(first)
    padded_one = extended(hidden_one, (("col", 3), ("row", 2)), 1)
    kernel = w_spatial.reshape((w_spatial.shape[0], 9) + w_spatial.shape[3:])
    second = jnp.einsum(
        "nkchw,nkcm->nmhw", taps(padded_one, height, breadth, False), kernel, precision=highest
    )
    second = second * stacked_channel(scale_two) + stacked_channel(shift_two)
    hidden_two = jax.nn.silu(second)
    third = jnp.einsum("nmhw,ncm->nchw", hidden_two, w_expand, precision=highest)
    third = third * stacked_channel(scale_three) + stacked_channel(shift_three)
    joined = inputs + third
    return (first, padded_one, second, hidden_two, joined)


def backward(inputs, upstream, saved, weights):
    w_reduce, w_spatial, w_expand, scale_one, shift_one, scale_two, shift_two, scale_three, shift_three = weights
    first, padded_one, second, hidden_two, joined = saved
    height, breadth = (inputs.shape[2], inputs.shape[3])
    grad_joined = upstream * silu_grad(joined)
    grad_third = grad_joined * per_channel(scale_three)
    grad_second = pointwise(grad_third, w_expand) * silu_grad(second) * per_channel(scale_two)
    padded_grad = extended(grad_second, (("col", 3), ("row", 2)), 1)
    grad_first = (
        spatial_back(padded_grad, w_spatial, height, breadth)
        * silu_grad(first)
        * per_channel(scale_one)
    )
    down_grad = grad_joined + pointwise_back(grad_first, w_reduce)
    return down_grad, (grad_third, grad_second, grad_first)


def weight_terms(inputs, saved, grads):
    first, padded_one, second, hidden_two, joined = saved
    grad_third, grad_second, grad_first = grads
    height, breadth = (inputs.shape[2], inputs.shape[3])
    expand_term = jnp.einsum("nmhw,nchw->nmc", hidden_two, grad_third, precision=highest)
    stacked = taps(padded_one, height, breadth, False)
    spatial_term = jnp.einsum("nkchw,nohw->nkco", stacked, grad_second, precision=highest)
    reduce_term = jnp.einsum("nchw,nmhw->ncm", inputs, grad_first, precision=highest)
    sections = inputs.shape[0]
    flat = jnp.concatenate(
        [t.reshape(sections, -1) for t in (reduce_term, spatial_term, expand_term)], axis=1
    )
    shapes = [reduce_term.shape[1:], (3, 3) + spatial_term.shape[2:], expand_term.shape[1:]]
    return flat, shapes


def gathered_weights(weights, sections):
    w_reduce, w_spatial, w_expand, scale_one, shift_one, scale_two, shift_two, scale_three, shift_three = (
        w[0] for w in weights
    )
    lanes = w_reduce.shape[1]
    rows = [
        w_reduce,
        w_spatial.reshape(-1, lanes),
        w_expand.T,
        jnp.stack([scale_one, shift_one, scale_two, shift_two]),
        scale_three.reshape(-1, lanes),
        shift_three.reshape(-1, lanes),
    ]
    flat = jnp.concatenate(rows)
    packed = jnp.broadcast_to(flat[None], (sections,) + flat.shape)
    every = lax.all_to_all(packed, "section", 0, 0, tiled=True)
    parts, offset = ([], 0)
    for r in rows:
        parts.append(every[:, offset : offset + r.shape[0]])
        offset += r.shape[0]
    small = parts[3]
    return (
        parts[0],
        parts[1].reshape((sections,) + w_spatial.shape),
        parts[2],
        small[:, 0],
        small[:, 1],
        small[:, 2],
        small[:, 3],
        parts[4].reshape(sections, -1),
        parts[5].reshape(sections, -1),
    )


def shifted_pieces(stacked, me, sections):
    pieces = [lax.dynamic_index_in_dim(stacked, me, axis=0, keepdims=False)]
    for d in range(1, sections):
        send = lax.dynamic_index_in_dim(stacked, (me + d) % sections, axis=0, keepdims=False)
        pairs = [(k, (k + d) % sections) for k in range(sections)]
        pieces.append(lax.ppermute(send, "section", pairs))
    return pieces


def reduced_terms(flat, shapes, me, sections, factor):
    flat = flat.reshape(sections, -1, 128)
    by_image = sum(shifted_pieces(flat, me, sections))
    group = lax.axis_size("row") * lax.axis_size("col")
    pieces = by_image.reshape(group, -1, 128)
    mine = lax.all_to_all(pieces, ("row", "col"), 0, 0, tiled=True).sum(axis=0) * factor
    copies = jnp.broadcast_to(mine[None], (group,) + mine.shape)
    total = lax.all_to_all(copies, ("row", "col"), 0, 0, tiled=True).reshape(-1)
    out, offset = ([], 0)
    for shape in shapes:
        size = 1
        for d in shape:
            size *= d
        out.append(total[offset : offset + size].reshape(shape))
        offset += size
    return out


def per_device(
    block_input,
    grad_out,
    w_reduce,
    w_spatial,
    w_expand,
    scale_one,
    shift_one,
    scale_two,
    shift_two,
    scale_three,
    shift_three,
):
    sections = lax.axis_size("section")
    me = lax.axis_index("section")
    images = block_input.shape[1]
    mine = lax.all_to_all(block_input[0], "section", 0, 0, tiled=True)
    gathered = gathered_weights(
        (w_reduce, w_spatial, w_expand, scale_one, shift_one, scale_two, shift_two, scale_three, shift_three),
        sections,
    )
    per_image = images // sections
    upstream = lax.dynamic_slice_in_dim(grad_out, me * per_image, per_image, axis=0)
    cells = images * mine.shape[2] * mine.shape[3] * lax.axis_size("row") * lax.axis_size("col")
    factor = 1.0 / jnp.sqrt(jnp.float32(cells))
    saved_all = forward(mine, gathered)
    down = [None] * sections
    grads = [None] * sections
    for sec in range(sections - 1, -1, -1):
        part = slice(sec * per_image, (sec + 1) * per_image)
        weights = tuple(g[sec] for g in gathered)
        saved = tuple(v[part] for v in saved_all)
        upstream, grads[sec] = backward(mine[part], upstream, saved, weights)
        down[sec] = upstream
    pieces = jnp.stack(shifted_pieces(jnp.stack(down), me, sections))
    order = (me - jnp.arange(sections)) % sections
    results = jnp.take(pieces, order, axis=0).reshape((images,) + mine.shape[1:])
    stacked_grads = tuple(jnp.concatenate([g[k] for g in grads]) for k in range(3))
    flat, shapes = weight_terms(mine, saved_all, stacked_grads)
    sums = reduced_terms(flat, shapes, me, sections, factor)
    return (results[None],) + tuple(t[None] for t in sums)


def solution(mesh):
    placed = (
        P("section", None, None, "row", "col"),
        P(None, None, "row", "col"),
        P("section", None, None),
        P("section", None, None, None, None),
        P("section", None, None),
        P("section", None),
        P("section", None),
        P("section", None),
        P("section", None),
        P("section", None),
        P("section", None),
    )
    return jax.shard_map(
        per_device,
        mesh=mesh,
        in_specs=placed,
        out_specs=(
            P("section", None, None, "row", "col"),
            P("section", None, None),
            P("section", None, None, None, None),
            P("section", None, None),
        ),
        check_vma=False,
    )
```
